512 devices in a mesh: tm: 16 (over z_hi, x), space: 32 (over y, z_lo, core).
Axes of the slice: x: 4, y: 4, z: 16 (z_hi: 4, z_lo: 4; z = z_hi * 4 + z_lo), core: 2. Of those that a mesh axis runs over, the one named last changes fastest.
Arguments:
- queries: bfloat16 [32, 4096, 1536], P('tm', 'space'), may hold values from -110 to 110
- keys: bfloat16 [32, 4096, 1536], P('tm', 'space'), may hold values from -5.1 to 5.1
- values: bfloat16 [32, 4096, 1536], P('tm', 'space'), may hold values from -15 to 15
- tile_mask: int32 [32, 32, 5, 5], P('tm', 'space'), may hold values from 0 to 1, as said below
Outputs:
- attended: bfloat16 [32, 4096, 1536], P('tm', 'space')
The draws below stay inside these ranges and needn't reach their ends.
Inputs may be any that keep to these rules, and one draw needn't show every extreme that they name: tile_mask[i, b, 2 + d, 2 + e] is 1 where tile (i, b) attends tile (i + d, b + e). It is 0 where |e| > 2 >> |d| or where the key tile lies outside the 32 x 32 tiles, and 1 for d = e = 0.
All inputs are finite; a program needn't handle non-finite values.
Results may differ from the reference program's by a relative error of at most 0.012.
Values may be sent and summed in bfloat16 or wider, within the bound.
No kernel may reach another device: no remote copies, remote signals or barrier semaphores. Data moves between devices by JAX's collectives and lax.ppermute only.
A program may use at most 192 MiB of HBM per device.

```python
import math
import jax
import jax.numpy as jnp
from jax import lax

H = 12
HD = 128
BLK = 128
TR = 2
W = 2
FRAMES = 32
NB = 32
ROWS = 4096


def key_field(key):
    shape = (FRAMES, ROWS, H * HD)
    base = jax.random.truncated_normal(jax.random.fold_in(key, 11), -5.0, 5.0, shape, jnp.float32)
    return base


def draw_keys(key, part):
    return key_field(key).astype(jnp.bfloat16)


def draw_queries(key, part):
    shape = (FRAMES, ROWS, H * HD)
    drawn = 2.0 * jax.random.truncated_normal(jax.random.fold_in(key, 13), -5.0, 5.0, shape, jnp.float32)
    return drawn.astype(jnp.bfloat16)


def draw_tile_mask(key, part):
    shape = (FRAMES, NB, 2 * TR + 1, 2 * W + 1)
    level_bits = jax.random.randint(jax.random.fold_in(key, 21), (FRAMES, 1, 1, 1), 0, 4)
    level = jnp.left_shift(jnp.ones_like(level_bits), level_bits)
    frame_index = jax.lax.broadcasted_iota(jnp.int32, shape, 0)
    block_index = jax.lax.broadcasted_iota(jnp.int32, shape, 1)
    d = jax.lax.broadcasted_iota(jnp.int32, shape, 2) - TR
    e = jax.lax.broadcasted_iota(jnp.int32, shape, 3) - W
    level = jnp.where(frame_index == FRAMES // 2, 8, level)
    draw_roll = jax.random.randint(jax.random.fold_in(key, 22), shape, 0, 8)
    kept = draw_roll < level
    inside_band = jnp.abs(e) <= jnp.right_shift(jnp.full(shape, W, jnp.int32), jnp.abs(d))
    valid = (frame_index + d >= 0) & (frame_index + d < FRAMES) & (block_index + e >= 0) & (block_index + e < NB)
    center = (d == 0) & (e == 0)
    return jnp.where(center | kept & inside_band & valid, 1, 0).astype(jnp.int32)


def shard_levels(key, dims, split, smallest, high):
    gain, own = 1.0, jax.random.fold_in(key, 6)
    for axis_at, shards_of in split:
        heights = jnp.exp(jax.random.uniform(jax.random.fold_in(own, axis_at), (shards_of,), jnp.float32, smallest / len(split), high / len(split)))
        gain = gain * jnp.repeat(heights, dims[axis_at] // shards_of).reshape([-1 if axis == axis_at else 1 for axis in range(len(dims))])
    return gain


def scatter_about(key, extent, scale, limit, shards=(), kind=jnp.bfloat16):
    values = scale * jax.random.normal(key, extent, jnp.float32)
    if shards:
        values = values * shard_levels(key, extent, shards, -0.22, 0.18)
    return jnp.clip(values, -limit, limit).astype(kind)


def setup_inputs(seed: int = 0) -> dict:
    key_list = jax.random.split(jax.random.key(seed), 5)
    return {
        "queries": draw_queries(jax.random.fold_in(key_list[4], 71), 0),
        "keys": draw_keys(jax.random.fold_in(key_list[4], 71), 0),
        "values": scatter_about(key_list[2], (FRAMES, ROWS, H * HD), 3.0, 15.0, ((0, 16), (1, 32))),
        "tile_mask": draw_tile_mask(jax.random.fold_in(key_list[4], 71), 0),
    }


def band_list():
    pairs = []
    for d in range(-TR, TR + 1):
        spread = W >> abs(d)
        for e in range(-spread, spread + 1):
            pairs.append((d, e))
    return pairs

def reference(queries, keys, values, tile_mask):
    score_scale = 1.0 / math.sqrt(HD)
    pairs = band_list()

    def one_frame(index):
        query = lax.dynamic_index_in_dim(queries, index, 0, keepdims=False)
        query = query.reshape(NB, BLK, H, HD).astype(jnp.float32)
        frame_flags = lax.dynamic_index_in_dim(tile_mask, index, 0, keepdims=False)
        score_list = []
        value_list = []
        for d, e in pairs:
            source = jnp.clip(index + d, 0, FRAMES - 1).astype(jnp.int32)
            key_frame = lax.dynamic_index_in_dim(keys, source, 0, keepdims=False).reshape(NB, BLK, H, HD)
            key_frame = jnp.roll(key_frame, -e, axis=0).astype(jnp.float32)
            value_frame = lax.dynamic_index_in_dim(values, source, 0, keepdims=False).reshape(NB, BLK, H, HD)
            value_frame = jnp.roll(value_frame, -e, axis=0).astype(jnp.float32)
            scores = jnp.einsum('bqhc,bkhc->bhqk', query, key_frame) * score_scale
            kept = frame_flags[:, TR + d, W + e] > 0
            scores = jnp.where(kept[:, None, None, None], scores, -jnp.inf)
            score_list.append(scores)
            value_list.append(value_frame)
        scores = jnp.concatenate(score_list, axis=3)
        row_max = lax.optimization_barrier(jnp.max(scores, axis=3, keepdims=True))
        weights = jnp.exp(scores - row_max)
        denominator = lax.optimization_barrier(jnp.sum(weights, axis=3))
        rounded = weights.astype(jnp.bfloat16).astype(jnp.float32)
        summed = jnp.zeros((NB, BLK, H, HD), jnp.float32)
        for number in range(len(pairs)):
            portion = rounded[..., number * BLK:(number + 1) * BLK]
            summed = summed + jnp.einsum('bhqk,bkhc->bqhc', portion, value_list[number])
        result = summed / jnp.transpose(denominator, (0, 2, 1))[..., None]
        return result.reshape(ROWS, H * HD).astype(jnp.bfloat16)
    return lax.map(one_frame, jnp.arange(FRAMES, dtype=jnp.int32))
```

```python
import math

import jax
import jax.numpy as jnp
from jax import lax
from jax.sharding import PartitionSpec as P

HD = 128
TR = 2
W = 2


def shifted(block, axis, distance):
    devices = range(lax.axis_size(axis))
    route = [(i - distance, i) for i in devices if i - distance in devices]
    return lax.ppermute(block, axis, route)


def band_list():
    pairs = []
    for d in range(-TR, TR + 1):
        spread = W >> abs(d)
        for e in range(-spread, spread + 1):
            pairs.append((d, e))
    return pairs


def frame_reach(e):
    best = 0
    for d in range(TR + 1):
        if W >> d >= abs(e):
            best = d
    return best


def swap_cores(block):
    devices = range(lax.axis_size("space"))
    return lax.ppermute(block, "space", [(i, i ^ 1) for i in devices])


def fetch_rows_first(stacked):
    frame_count = stacked.shape[1]
    earlier = shifted(stacked[:, frame_count - TR :], "tm", 1)
    following = shifted(stacked[:, :TR], "tm", -1)
    far_next = shifted(stacked, "space", -2)
    far_prev = shifted(stacked, "space", 2)
    core_zero = lax.axis_index("space") % 2 == 0
    partner_own = swap_cores(stacked)
    partner_far = swap_cores(jnp.where(core_zero, far_next, far_prev))
    nearby = {
        0: stacked,
        2: far_next,
        -2: far_prev,
        1: jnp.where(core_zero, partner_own, partner_far),
        -1: jnp.where(core_zero, partner_far, partner_own),
    }
    band = jnp.concatenate([earlier[:, TR - 1 :], following[:, :1]], axis=1)
    diagonal = {1: shifted(band, "space", -1), -1: shifted(band, "space", 1)}
    columns = {}
    for e in range(-W, W + 1):
        extent = frame_reach(e)
        if e == 0:
            parts = [earlier, nearby[0], following]
        elif extent > 0:
            parts = [diagonal[e][:, :1], nearby[e], diagonal[e][:, 1:]]
        else:
            parts = [nearby[e]]
        columns[e] = jnp.concatenate(parts, axis=1)
    return columns


def attend(queries, columns, tile_flags):
    frame_count, row_count, feature_width = queries.shape
    head_count = feature_width // HD
    head_group = 4
    span = head_group * HD
    score_scale = 1.0 / math.sqrt(HD)
    pairs = band_list()
    outputs = []
    for index in range(head_count // head_group):
        first_col = index * span
        query = queries[:, :, first_col : first_col + span].reshape(
            frame_count, row_count, head_group, HD
        )
        score_list = []
        value_list = []
        kept_list = []
        for d, e in pairs:
            start = d + frame_reach(e)
            key_tile = columns[e][:, start : start + frame_count, :, first_col : first_col + span]
            key_tile = key_tile.reshape(2, frame_count, row_count, head_group, HD)
            kept = tile_flags[:, TR + d, W + e] > 0

            def compute(query=query, key_tile=key_tile, kept=kept):
                raw = (
                    jnp.einsum(
                        "fqhc,fkhc->fhqk", query, key_tile[0], preferred_element_type=jnp.float32
                    )
                    * score_scale
                )
                return jnp.where(kept[:, None, None, None], raw, -jnp.inf)

            scores = compute()
            score_list.append(scores)
            value_list.append(key_tile[1])
            kept_list.append(kept)
        row_max = jnp.max(score_list[0], axis=3, keepdims=True)
        for scores in score_list[1:]:
            row_max = jnp.maximum(row_max, jnp.max(scores, axis=3, keepdims=True))
        denominator = jnp.zeros((frame_count, head_group, row_count), jnp.float32)
        summed = jnp.zeros((frame_count, row_count, head_group, HD), jnp.float32)
        for number in range(len(pairs)):
            weights = jnp.exp(score_list[number] - row_max)
            denominator = denominator + jnp.sum(weights, axis=3)
            rounded = weights.astype(jnp.bfloat16)

            def product(portion=rounded, value_tile=value_list[number]):
                return jnp.einsum(
                    "fhqk,fkhc->fqhc", portion, value_tile, preferred_element_type=jnp.float32
                )

            summed = summed + product()
        result = summed / jnp.transpose(denominator, (0, 2, 1))[..., None]
        outputs.append(result.reshape(frame_count, row_count, span))
    return jnp.concatenate(outputs, axis=2).astype(jnp.bfloat16)


def on_device(queries, keys, values, tile_mask):
    stacked = jnp.stack([keys, values], 0)
    columns = fetch_rows_first(stacked)
    tile_flags = tile_mask[:, 0]
    return attend(queries, columns, tile_flags)


def solution(mesh):
    in_specs = (
        P("tm", "space", None),
        P("tm", "space", None),
        P("tm", "space", None),
        P("tm", "space", None, None),
    )
    out_specs = P("tm", "space", None)
    return jax.shard_map(
        on_device, mesh=mesh, in_specs=in_specs, out_specs=out_specs, check_vma=False
    )
```

```python
import math

import jax
import jax.numpy as jnp
from jax import lax
from jax.experimental import pallas as pl
from jax.experimental.pallas import tpu as pltpu
from jax.sharding import PartitionSpec as P

HD = 128
TR = 2
W = 2


def shifted(block, axis, distance):
    devices = range(lax.axis_size(axis))
    route = [(i - distance, i) for i in devices if i - distance in devices]
    return lax.ppermute(block, axis, route)


def band_list():
    pairs = []
    for d in range(-TR, TR + 1):
        spread = W >> abs(d)
        for e in range(-spread, spread + 1):
            pairs.append((d, e))
    return pairs


def frame_reach(e):
    best = 0
    for d in range(TR + 1):
        if W >> d >= abs(e):
            best = d
    return best


def swap_cores(block):
    devices = range(lax.axis_size("space"))
    return lax.ppermute(block, "space", [(i, i ^ 1) for i in devices])


def fetch_sources(stacked):
    frame_count = stacked.shape[1]
    earlier = shifted(stacked[:, frame_count - TR :], "tm", 1)
    following = shifted(stacked[:, :TR], "tm", -1)
    far_next = shifted(stacked, "space", -2)
    far_prev = shifted(stacked, "space", 2)
    core_zero = lax.axis_index("space") % 2 == 0
    partner_own = swap_cores(stacked)
    partner_far = swap_cores(jnp.where(core_zero, far_next, far_prev))
    near_next = jnp.where(core_zero, partner_own, partner_far)
    near_prev = jnp.where(core_zero, partner_far, partner_own)
    band = jnp.concatenate([earlier[:, TR - 1 :], following[:, :1]], axis=1)
    diag_next = shifted(band, "space", -1)
    diag_prev = shifted(band, "space", 1)
    return (stacked, earlier, following, far_next, far_prev, near_next, near_prev, diag_next, diag_prev)


def locate(frame, d, e):
    offset = frame + d
    if e == 0:
        if offset < 0:
            return 1, offset + TR
        if offset < 2:
            return 0, offset
        return 2, offset - 2
    if abs(e) == 1:
        near, diag = (5, 7) if e > 0 else (6, 8)
        if offset < 0:
            return diag, 0
        if offset < 2:
            return near, offset
        return diag, 1
    return (3 if e > 0 else 4), frame


def attention_kernel(flags_ref, q_ref, *refs):
    *sources, o_ref = refs
    frame_count = q_ref.shape[0]
    score_scale = 1.0 / math.sqrt(HD)
    for frame in range(frame_count):
        query = q_ref[frame]
        score_list = []
        value_list = []
        for d, e in band_list():
            which, index = locate(frame, d, e)
            key_tile = sources[which][0, index]
            raw = (
                lax.dot_general(
                    query, key_tile, (((1,), (1,)), ((), ())), preferred_element_type=jnp.float32
                )
                * score_scale
            )
            flag = flags_ref[frame * 25 + (TR + d) * 5 + (W + e)]
            score_list.append(jnp.where(flag > 0, raw, -jnp.inf))
            value_list.append(sources[which][1, index])
        row_max = jnp.max(score_list[0], axis=1, keepdims=True)
        for scores in score_list[1:]:
            row_max = jnp.maximum(row_max, jnp.max(scores, axis=1, keepdims=True))
        denominator = jnp.zeros_like(row_max)
        summed = jnp.zeros((query.shape[0], HD), jnp.float32)
        for scores, value_tile in zip(score_list, value_list):
            weights = jnp.exp(scores - row_max)
            denominator = denominator + jnp.sum(weights, axis=1, keepdims=True)
            summed = summed + jnp.dot(
                weights.astype(jnp.bfloat16), value_tile, preferred_element_type=jnp.float32
            )
        o_ref[frame] = (summed / denominator).astype(o_ref.dtype)


def attend(queries, sources, tile_flags):
    frame_count, row_count, feature_width = queries.shape
    head_count = feature_width // HD
    flags = tile_flags.reshape(-1).astype(jnp.int32)
    source_spec = pl.BlockSpec((2, 2, row_count, HD), lambda h, flags: (0, 0, 0, h))
    tile_spec = pl.BlockSpec((frame_count, row_count, HD), lambda h, flags: (0, 0, h))
    grid_spec = pltpu.PrefetchScalarGridSpec(
        num_scalar_prefetch=1,
        grid=(head_count,),
        in_specs=[tile_spec] + [source_spec] * len(sources),
        out_specs=tile_spec,
    )
    pairs = len(band_list())
    cost = pl.CostEstimate(
        flops=4 * frame_count * head_count * pairs * row_count * row_count * HD,
        transcendentals=frame_count * head_count * pairs * row_count * row_count,
        bytes_accessed=(2 + 4 * len(sources)) * frame_count * row_count * feature_width,
    )
    return pl.pallas_call(
        attention_kernel,
        grid_spec=grid_spec,
        out_shape=jax.ShapeDtypeStruct(queries.shape, queries.dtype),
        cost_estimate=cost,
    )(flags, queries, *sources)


def on_device(queries, keys, values, tile_mask):
    stacked = jnp.stack([keys, values], 0)
    sources = fetch_sources(stacked)
    tile_flags = tile_mask[:, 0]
    return attend(queries, sources, tile_flags)


def solution(mesh):
    in_specs = (
        P("tm", "space", None),
        P("tm", "space", None),
        P("tm", "space", None),
        P("tm", "space", None, None),
    )
    out_specs = P("tm", "space", None)
    return jax.shard_map(
        on_device, mesh=mesh, in_specs=in_specs, out_specs=out_specs, check_vma=False
    )
```

```python
import math

import jax
import jax.numpy as jnp
from jax import lax
from jax.experimental import pallas as pl
from jax.experimental.pallas import tpu as pltpu
from jax.sharding import PartitionSpec as P

HD = 128
TR = 2
W = 2


def shifted(block, axis, distance):
    devices = range(lax.axis_size(axis))
    route = [(i - distance, i) for i in devices if i - distance in devices]
    return lax.ppermute(block, axis, route)


def band_list():
    pairs = []
    for d in range(-TR, TR + 1):
        spread = W >> abs(d)
        for e in range(-spread, spread + 1):
            pairs.append((d, e))
    return pairs


def frame_reach(e):
    best = 0
    for d in range(TR + 1):
        if W >> d >= abs(e):
            best = d
    return best


def swap_cores(block):
    devices = range(lax.axis_size("space"))
    return lax.ppermute(block, "space", [(i, i ^ 1) for i in devices])


def fetch_sources(stacked):
    frame_count = stacked.shape[1]
    earlier = shifted(stacked[:, frame_count - TR :], "tm", 1)
    following = shifted(stacked[:, :TR], "tm", -1)
    far_next = shifted(stacked, "space", -2)
    far_prev = shifted(stacked, "space", 2)
    core_zero = lax.axis_index("space") % 2 == 0
    partner_own = swap_cores(stacked)
    partner_far = swap_cores(jnp.where(core_zero, far_next, far_prev))
    near_next = jnp.where(core_zero, partner_own, partner_far)
    near_prev = jnp.where(core_zero, partner_far, partner_own)
    last, first = slice(frame_count - 1, frame_count), slice(0, 1)
    diag_earlier = shifted(
        jnp.concatenate([near_next[:, last], near_prev[:, last]], axis=1), "tm", 1
    )
    diag_following = shifted(
        jnp.concatenate([near_next[:, first], near_prev[:, first]], axis=1), "tm", -1
    )
    return (
        stacked, earlier, following, far_next, far_prev, near_next, near_prev, diag_earlier,
        diag_following,
    )


def locate(frame, d, e):
    offset = frame + d
    if e == 0:
        if offset < 0:
            return 1, offset + TR
        if offset < 2:
            return 0, offset
        return 2, offset - 2
    if abs(e) == 1:
        side = 0 if e > 0 else 1
        if offset < 0:
            return 7, side
        if offset < 2:
            return 5 + side, offset
        return 8, side
    return (3 if e > 0 else 4), frame


def attention_kernel(flags_ref, q_ref, *refs):
    *sources, o_ref = refs
    frame_count = q_ref.shape[0]
    score_scale = 1.0 / math.sqrt(HD)
    for frame in range(frame_count):
        query = q_ref[frame]
        score_list = []
        value_list = []
        for d, e in band_list():
            which, index = locate(frame, d, e)
            key_tile = sources[which][0, index]
            raw = (
                lax.dot_general(
                    query, key_tile, (((1,), (1,)), ((), ())), preferred_element_type=jnp.float32
                )
                * score_scale
            )
            flag = flags_ref[frame * 25 + (TR + d) * 5 + (W + e)]
            score_list.append(jnp.where(flag > 0, raw, -jnp.inf))
            value_list.append(sources[which][1, index])
        row_max = jnp.max(score_list[0], axis=1, keepdims=True)
        for scores in score_list[1:]:
            row_max = jnp.maximum(row_max, jnp.max(scores, axis=1, keepdims=True))
        denominator = jnp.zeros_like(row_max)
        summed = jnp.zeros((query.shape[0], HD), jnp.float32)
        for scores, value_tile in zip(score_list, value_list):
            weights = jnp.exp(scores - row_max)
            denominator = denominator + jnp.sum(weights, axis=1, keepdims=True)
            summed = summed + jnp.dot(
                weights.astype(jnp.bfloat16), value_tile, preferred_element_type=jnp.float32
            )
        o_ref[frame] = (summed / denominator).astype(o_ref.dtype)


def attend(queries, sources, tile_flags):
    frame_count, row_count, feature_width = queries.shape
    head_count = feature_width // HD
    flags = tile_flags.reshape(-1).astype(jnp.int32)
    source_spec = pl.BlockSpec((2, 2, row_count, HD), lambda h, flags: (0, 0, 0, h))
    tile_spec = pl.BlockSpec((frame_count, row_count, HD), lambda h, flags: (0, 0, h))
    grid_spec = pltpu.PrefetchScalarGridSpec(
        num_scalar_prefetch=1,
        grid=(head_count,),
        in_specs=[tile_spec] + [source_spec] * len(sources),
        out_specs=tile_spec,
    )
    pairs = len(band_list())
    cost = pl.CostEstimate(
        flops=4 * frame_count * head_count * pairs * row_count * row_count * HD,
        transcendentals=frame_count * head_count * pairs * row_count * row_count,
        bytes_accessed=(2 + 4 * len(sources)) * frame_count * row_count * feature_width,
    )
    return pl.pallas_call(
        attention_kernel,
        grid_spec=grid_spec,
        out_shape=jax.ShapeDtypeStruct(queries.shape, queries.dtype),
        cost_estimate=cost,
    )(flags, queries, *sources)


def on_device(queries, keys, values, tile_mask):
    stacked = jnp.stack([keys, values], 0)
    sources = fetch_sources(stacked)
    tile_flags = tile_mask[:, 0]
    return attend(queries, sources, tile_flags)


def solution(mesh):
    in_specs = (
        P("tm", "space", None),
        P("tm", "space", None),
        P("tm", "space", None),
        P("tm", "space", None, None),
    )
    out_specs = P("tm", "space", None)
    return jax.shard_map(
        on_device, mesh=mesh, in_specs=in_specs, out_specs=out_specs, check_vma=False
    )
```

```python
import math

import jax
import jax.numpy as jnp
from jax import lax
from jax.experimental import pallas as pl
from jax.experimental.pallas import tpu as pltpu
from jax.sharding import PartitionSpec as P

HD = 128
TR = 2
W = 2


def shifted(block, axis, distance):
    devices = range(lax.axis_size(axis))
    route = [(i - distance, i) for i in devices if i - distance in devices]
    return lax.ppermute(block, axis, route)


def band_list():
    pairs = []
    for d in range(-TR, TR + 1):
        spread = W >> abs(d)
        for e in range(-spread, spread + 1):
            pairs.append((d, e))
    return pairs


def frame_reach(e):
    best = 0
    for d in range(TR + 1):
        if W >> d >= abs(e):
            best = d
    return best


X_CHIPS = 4


def routed(pairs, block, axis="tm"):
    return lax.ppermute(block, axis, pairs) if pairs else jnp.zeros_like(block)


def tm_shift(block, step):
    count = lax.axis_size("tm")
    if step > 0:
        edge = [t for t in range(count - 1) if t % X_CHIPS == X_CHIPS - 1]
        direct = [(t, t + 1) for t in range(count - 1) if t not in edge]
        x_then_z = ([(t, t - X_CHIPS + 1) for t in edge], [(t - X_CHIPS + 1, t + 1) for t in edge])
        z_then_x = ([(t, t + X_CHIPS) for t in edge], [(t + X_CHIPS, t + 1) for t in edge])
    else:
        edge = [t for t in range(1, count) if t % X_CHIPS == 0]
        direct = [(t, t - 1) for t in range(1, count) if t not in edge]
        x_then_z = ([(t, t + X_CHIPS - 1) for t in edge], [(t + X_CHIPS - 1, t - 1) for t in edge])
        z_then_x = ([(t, t - X_CHIPS) for t in edge], [(t - X_CHIPS, t - 1) for t in edge])
    plain = routed(direct, block)
    first = routed(x_then_z[1], routed(x_then_z[0], block[:1]))
    second = routed(z_then_x[1], routed(z_then_x[0], block[1:]))
    position = lax.axis_index("tm") % X_CHIPS
    at_edge = position == (0 if step > 0 else X_CHIPS - 1)
    return jnp.where(at_edge, jnp.concatenate([first, second], axis=0), plain)


def swap_cores(block):
    devices = range(lax.axis_size("space"))
    return lax.ppermute(block, "space", [(i, i ^ 1) for i in devices])


def fetch_sources(stacked):
    frame_count = stacked.shape[1]
    earlier = tm_shift(stacked[:, frame_count - TR :], 1)
    following = tm_shift(stacked[:, :TR], -1)
    far_next = shifted(stacked, "space", -2)
    far_prev = shifted(stacked, "space", 2)
    core_zero = lax.axis_index("space") % 2 == 0
    partner_own = swap_cores(stacked)
    partner_far = swap_cores(jnp.where(core_zero, far_next, far_prev))
    near_next = jnp.where(core_zero, partner_own, partner_far)
    near_prev = jnp.where(core_zero, partner_far, partner_own)
    band = jnp.concatenate([earlier[:, TR - 1 :], following[:, :1]], axis=1)
    diag_next = shifted(band, "space", -1)
    diag_prev = shifted(band, "space", 1)
    return (stacked, earlier, following, far_next, far_prev, near_next, near_prev, diag_next, diag_prev)


def locate(frame, d, e):
    offset = frame + d
    if e == 0:
        if offset < 0:
            return 1, offset + TR
        if offset < 2:
            return 0, offset
        return 2, offset - 2
    if abs(e) == 1:
        near, diag = (5, 7) if e > 0 else (6, 8)
        if offset < 0:
            return diag, 0
        if offset < 2:
            return near, offset
        return diag, 1
    return (3 if e > 0 else 4), frame


def attention_kernel(flags_ref, q_ref, *refs):
    *sources, o_ref = refs
    frame_count = q_ref.shape[0]
    score_scale = 1.0 / math.sqrt(HD)
    for frame in range(frame_count):
        query = q_ref[frame]
        score_list = []
        value_list = []
        for d, e in band_list():
            which, index = locate(frame, d, e)
            key_tile = sources[which][0, index]
            raw = (
                lax.dot_general(
                    query, key_tile, (((1,), (1,)), ((), ())), preferred_element_type=jnp.float32
                )
                * score_scale
            )
            flag = flags_ref[frame * 25 + (TR + d) * 5 + (W + e)]
            score_list.append(jnp.where(flag > 0, raw, -jnp.inf))
            value_list.append(sources[which][1, index])
        row_max = jnp.max(score_list[0], axis=1, keepdims=True)
        for scores in score_list[1:]:
            row_max = jnp.maximum(row_max, jnp.max(scores, axis=1, keepdims=True))
        denominator = jnp.zeros_like(row_max)
        summed = jnp.zeros((query.shape[0], HD), jnp.float32)
        for scores, value_tile in zip(score_list, value_list):
            weights = jnp.exp(scores - row_max)
            denominator = denominator + jnp.sum(weights, axis=1, keepdims=True)
            summed = summed + jnp.dot(
                weights.astype(jnp.bfloat16), value_tile, preferred_element_type=jnp.float32
            )
        o_ref[frame] = (summed / denominator).astype(o_ref.dtype)


def attend(queries, sources, tile_flags):
    frame_count, row_count, feature_width = queries.shape
    head_count = feature_width // HD
    flags = tile_flags.reshape(-1).astype(jnp.int32)
    source_spec = pl.BlockSpec((2, 2, row_count, HD), lambda h, flags: (0, 0, 0, h))
    tile_spec = pl.BlockSpec((frame_count, row_count, HD), lambda h, flags: (0, 0, h))
    grid_spec = pltpu.PrefetchScalarGridSpec(
        num_scalar_prefetch=1,
        grid=(head_count,),
        in_specs=[tile_spec] + [source_spec] * len(sources),
        out_specs=tile_spec,
    )
    pairs = len(band_list())
    cost = pl.CostEstimate(
        flops=4 * frame_count * head_count * pairs * row_count * row_count * HD,
        transcendentals=frame_count * head_count * pairs * row_count * row_count,
        bytes_accessed=(2 + 4 * len(sources)) * frame_count * row_count * feature_width,
    )
    return pl.pallas_call(
        attention_kernel,
        grid_spec=grid_spec,
        out_shape=jax.ShapeDtypeStruct(queries.shape, queries.dtype),
        cost_estimate=cost,
    )(flags, queries, *sources)


def on_device(queries, keys, values, tile_mask):
    stacked = jnp.stack([keys, values], 0)
    sources = fetch_sources(stacked)
    tile_flags = tile_mask[:, 0]
    return attend(queries, sources, tile_flags)


def solution(mesh):
    in_specs = (
        P("tm", "space", None),
        P("tm", "space", None),
        P("tm", "space", None),
        P("tm", "space", None, None),
    )
    out_specs = P("tm", "space", None)
    return jax.shard_map(
        on_device, mesh=mesh, in_specs=in_specs, out_specs=out_specs, check_vma=False
    )
```

```python
import math

import jax
import jax.numpy as jnp
from jax import lax
from jax.experimental import pallas as pl
from jax.experimental.pallas import tpu as pltpu
from jax.sharding import PartitionSpec as P

HD = 128
TR = 2
W = 2


def shifted(block, axis, distance):
    devices = range(lax.axis_size(axis))
    route = [(i - distance, i) for i in devices if i - distance in devices]
    return lax.ppermute(block, axis, route)


def band_list():
    pairs = []
    for d in range(-TR, TR + 1):
        spread = W >> abs(d)
        for e in range(-spread, spread + 1):
            pairs.append((d, e))
    return pairs


def frame_reach(e):
    best = 0
    for d in range(TR + 1):
        if W >> d >= abs(e):
            best = d
    return best


def swap_cores(block):
    devices = range(lax.axis_size("space"))
    return lax.ppermute(block, "space", [(i, i ^ 1) for i in devices])


def fetch_sources(stacked):
    frame_count = stacked.shape[1]
    earlier = shifted(stacked[:, frame_count - TR :], "tm", 1)
    following = shifted(stacked[:, :TR], "tm", -1)
    far_next = shifted(stacked, "space", -2)
    far_prev = shifted(stacked, "space", 2)
    core_zero = lax.axis_index("space") % 2 == 0
    partner_own = swap_cores(stacked)
    partner_far = swap_cores(jnp.where(core_zero, far_next, far_prev))
    near_next = jnp.where(core_zero, partner_own, partner_far)
    near_prev = jnp.where(core_zero, partner_far, partner_own)
    band = jnp.concatenate([earlier[:, TR - 1 :], following[:, :1]], axis=1)
    diag_next = shifted(band, "space", -1)
    diag_prev = shifted(band, "space", 1)
    return (stacked, earlier, following, far_next, far_prev, near_next, near_prev, diag_next, diag_prev)


def locate(frame, d, e):
    offset = frame + d
    if e == 0:
        if offset < 0:
            return 1, offset + TR
        if offset < 2:
            return 0, offset
        return 2, offset - 2
    if abs(e) == 1:
        near, diag = (5, 7) if e > 0 else (6, 8)
        if offset < 0:
            return diag, 0
        if offset < 2:
            return near, offset
        return diag, 1
    return (3 if e > 0 else 4), frame


LOCAL = (0, 3, 4, 5, 6)
REMOTE = (1, 2, 7, 8)


def scored_pairs(flags_ref, query, sources, frame, kept_sources):
    score_scale = 1.0 / math.sqrt(HD)
    score_list = []
    value_list = []
    for d, e in band_list():
        which, index = locate(frame, d, e)
        if which not in kept_sources:
            continue
        source = sources[kept_sources.index(which)]
        raw = (
            lax.dot_general(
                query, source[0, index], (((1,), (1,)), ((), ())), preferred_element_type=jnp.float32
            )
            * score_scale
        )
        flag = flags_ref[frame * 25 + (TR + d) * 5 + (W + e)]
        score_list.append(jnp.where(flag > 0, raw, -jnp.inf))
        value_list.append(source[1, index])
    row_max = jnp.max(score_list[0], axis=1, keepdims=True)
    for scores in score_list[1:]:
        row_max = jnp.maximum(row_max, jnp.max(scores, axis=1, keepdims=True))
    return score_list, value_list, row_max


def weighted_sums(score_list, value_list, row_max):
    denominator = jnp.zeros_like(row_max)
    summed = jnp.zeros((row_max.shape[0], HD), jnp.float32)
    for scores, value_tile in zip(score_list, value_list):
        weights = jnp.exp(scores - row_max)
        denominator = denominator + jnp.sum(weights, axis=1, keepdims=True)
        summed = summed + jnp.dot(
            weights.astype(jnp.bfloat16), value_tile, preferred_element_type=jnp.float32
        )
    return denominator, summed


def local_kernel(flags_ref, q_ref, *refs):
    *sources, max_ref, sum_ref, acc_ref = refs
    for frame in range(q_ref.shape[0]):
        score_list, value_list, row_max = scored_pairs(
            flags_ref, q_ref[frame], sources, frame, LOCAL
        )
        denominator, summed = weighted_sums(score_list, value_list, row_max)
        max_ref[0, frame] = row_max
        sum_ref[0, frame] = denominator
        acc_ref[frame] = summed


def remote_kernel(flags_ref, q_ref, *refs):
    *sources, max_ref, sum_ref, acc_ref, o_ref = refs
    for frame in range(q_ref.shape[0]):
        score_list, value_list, remote_max = scored_pairs(
            flags_ref, q_ref[frame], sources, frame, REMOTE
        )
        local_max = max_ref[0, frame]
        row_max = jnp.maximum(local_max, remote_max)
        rescale = jnp.exp(local_max - row_max)
        denominator, summed = weighted_sums(score_list, value_list, row_max)
        denominator = denominator + rescale * sum_ref[0, frame]
        summed = summed + rescale * acc_ref[frame]
        o_ref[frame] = (summed / denominator).astype(o_ref.dtype)


def attend(queries, sources, tile_flags):
    frame_count, row_count, feature_width = queries.shape
    head_count = feature_width // HD
    flags = tile_flags.reshape(-1).astype(jnp.int32)
    source_spec = pl.BlockSpec((2, 2, row_count, HD), lambda h, flags: (0, 0, 0, h))
    tile_spec = pl.BlockSpec((frame_count, row_count, HD), lambda h, flags: (0, 0, h))
    stat_spec = pl.BlockSpec((1, frame_count, row_count, 1), lambda h, flags: (h, 0, 0, 0))
    stat_shape = jax.ShapeDtypeStruct((head_count, frame_count, row_count, 1), jnp.float32)
    acc_shape = jax.ShapeDtypeStruct(queries.shape, jnp.float32)
    local_sources = [sources[i] for i in LOCAL]
    remote_sources = [sources[i] for i in REMOTE]

    def cost(count, extra):
        return pl.CostEstimate(
            flops=4 * frame_count * head_count * count * row_count * row_count * HD,
            transcendentals=frame_count * head_count * count * row_count * row_count,
            bytes_accessed=(2 + 4 * extra + 4) * frame_count * row_count * feature_width,
        )

    stats = pl.pallas_call(
        local_kernel,
        grid_spec=pltpu.PrefetchScalarGridSpec(
            num_scalar_prefetch=1,
            grid=(head_count,),
            in_specs=[tile_spec] + [source_spec] * len(local_sources),
            out_specs=[stat_spec, stat_spec, tile_spec],
        ),
        out_shape=[stat_shape, stat_shape, acc_shape],
        cost_estimate=cost(16, len(local_sources)),
    )(flags, queries, *local_sources)
    return pl.pallas_call(
        remote_kernel,
        grid_spec=pltpu.PrefetchScalarGridSpec(
            num_scalar_prefetch=1,
            grid=(head_count,),
            in_specs=[tile_spec] + [source_spec] * len(remote_sources)
            + [stat_spec, stat_spec, tile_spec],
            out_specs=tile_spec,
        ),
        out_shape=jax.ShapeDtypeStruct(queries.shape, queries.dtype),
        cost_estimate=cost(10, len(remote_sources)),
    )(flags, queries, *remote_sources, *stats)


def on_device(queries, keys, values, tile_mask):
    stacked = jnp.stack([keys, values], 0)
    sources = fetch_sources(stacked)
    tile_flags = tile_mask[:, 0]
    return attend(queries, sources, tile_flags)


def solution(mesh):
    in_specs = (
        P("tm", "space", None),
        P("tm", "space", None),
        P("tm", "space", None),
        P("tm", "space", None, None),
    )
    out_specs = P("tm", "space", None)
    return jax.shard_map(
        on_device, mesh=mesh, in_specs=in_specs, out_specs=out_specs, check_vma=False
    )
```

```python
import math

import jax
import jax.numpy as jnp
from jax import lax
from jax.experimental import pallas as pl
from jax.experimental.pallas import tpu as pltpu
from jax.sharding import PartitionSpec as P

HD = 128
TR = 2
W = 2


def shifted(block, axis, distance):
    devices = range(lax.axis_size(axis))
    route = [(i - distance, i) for i in devices if i - distance in devices]
    return lax.ppermute(block, axis, route)


def band_list():
    pairs = []
    for d in range(-TR, TR + 1):
        spread = W >> abs(d)
        for e in range(-spread, spread + 1):
            pairs.append((d, e))
    return pairs


def frame_reach(e):
    best = 0
    for d in range(TR + 1):
        if W >> d >= abs(e):
            best = d
    return best


def swap_cores(block):
    devices = range(lax.axis_size("space"))
    return lax.ppermute(block, "space", [(i, i ^ 1) for i in devices])


def fetch_sources(stacked):
    frame_count = stacked.shape[1]
    earlier = shifted(stacked[:, frame_count - TR :], "tm", 1)
    following = shifted(stacked[:, :TR], "tm", -1)
    far_next = shifted(stacked, "space", -2)
    far_prev = shifted(stacked, "space", 2)
    core_zero = lax.axis_index("space") % 2 == 0
    partner_own = swap_cores(stacked)
    partner_far = swap_cores(jnp.where(core_zero, far_next, far_prev))
    near_next = jnp.where(core_zero, partner_own, partner_far)
    near_prev = jnp.where(core_zero, partner_far, partner_own)
    band = jnp.concatenate([earlier[:, TR - 1 :], following[:, :1]], axis=1)
    diag_next = shifted(band, "space", -1)
    diag_prev = shifted(band, "space", 1)
    return (stacked, earlier, following, far_next, far_prev, near_next, near_prev, diag_next, diag_prev)


def locate(frame, d, e):
    offset = frame + d
    if e == 0:
        if offset < 0:
            return 1, offset + TR
        if offset < 2:
            return 0, offset
        return 2, offset - 2
    if abs(e) == 1:
        near, diag = (5, 7) if e > 0 else (6, 8)
        if offset < 0:
            return diag, 0
        if offset < 2:
            return near, offset
        return diag, 1
    return (3 if e > 0 else 4), frame


LOCAL = (0, 3, 4, 5, 6)
HEAD_GROUP = 4
REMOTE = (1, 2, 7, 8)


def scored_pairs(flags_ref, query, sources, frame, kept_sources, lanes):
    score_scale = 1.0 / math.sqrt(HD)
    score_list = []
    value_list = []
    for d, e in band_list():
        which, index = locate(frame, d, e)
        if which not in kept_sources:
            continue
        source = sources[kept_sources.index(which)]
        raw = (
            lax.dot_general(
                query, source[0, index, :, lanes], (((1,), (1,)), ((), ())),
                preferred_element_type=jnp.float32,
            )
            * score_scale
        )
        flag = flags_ref[frame * 25 + (TR + d) * 5 + (W + e)]
        score_list.append(jnp.where(flag > 0, raw, -jnp.inf))
        value_list.append(source[1, index, :, lanes])
    row_max = jnp.max(score_list[0], axis=1, keepdims=True)
    for scores in score_list[1:]:
        row_max = jnp.maximum(row_max, jnp.max(scores, axis=1, keepdims=True))
    return score_list, value_list, row_max


def weighted_sums(score_list, value_list, row_max):
    denominator = jnp.zeros_like(row_max)
    summed = jnp.zeros((row_max.shape[0], HD), jnp.float32)
    for scores, value_tile in zip(score_list, value_list):
        weights = jnp.exp(scores - row_max)
        denominator = denominator + jnp.sum(weights, axis=1, keepdims=True)
        summed = summed + jnp.dot(
            weights.astype(jnp.bfloat16), value_tile, preferred_element_type=jnp.float32
        )
    return denominator, summed


def local_kernel(flags_ref, q_ref, *refs):
    *sources, max_ref, sum_ref, acc_ref = refs
    for head in range(max_ref.shape[0]):
        lanes = slice(head * HD, (head + 1) * HD)
        for frame in range(q_ref.shape[0]):
            score_list, value_list, row_max = scored_pairs(
                flags_ref, q_ref[frame, :, lanes], sources, frame, LOCAL, lanes
            )
            denominator, summed = weighted_sums(score_list, value_list, row_max)
            max_ref[head, frame] = row_max
            sum_ref[head, frame] = denominator
            acc_ref[frame, :, lanes] = summed


def remote_kernel(flags_ref, q_ref, *refs):
    *sources, max_ref, sum_ref, acc_ref, o_ref = refs
    for head in range(max_ref.shape[0]):
        lanes = slice(head * HD, (head + 1) * HD)
        for frame in range(q_ref.shape[0]):
            score_list, value_list, remote_max = scored_pairs(
                flags_ref, q_ref[frame, :, lanes], sources, frame, REMOTE, lanes
            )
            local_max = max_ref[head, frame]
            row_max = jnp.maximum(local_max, remote_max)
            rescale = jnp.exp(local_max - row_max)
            denominator, summed = weighted_sums(score_list, value_list, row_max)
            denominator = denominator + rescale * sum_ref[head, frame]
            summed = summed + rescale * acc_ref[frame, :, lanes]
            o_ref[frame, :, lanes] = (summed / denominator).astype(o_ref.dtype)


def attend(queries, sources, tile_flags):
    frame_count, row_count, feature_width = queries.shape
    head_count = feature_width // HD
    group = HEAD_GROUP
    steps = head_count // group
    flags = tile_flags.reshape(-1).astype(jnp.int32)
    source_spec = pl.BlockSpec((2, 2, row_count, group * HD), lambda h, flags: (0, 0, 0, h))
    tile_spec = pl.BlockSpec((frame_count, row_count, group * HD), lambda h, flags: (0, 0, h))
    stat_spec = pl.BlockSpec((group, frame_count, row_count, 1), lambda h, flags: (h, 0, 0, 0))
    stat_shape = jax.ShapeDtypeStruct((head_count, frame_count, row_count, 1), jnp.float32)
    acc_shape = jax.ShapeDtypeStruct(queries.shape, jnp.float32)
    local_sources = [sources[i] for i in LOCAL]
    remote_sources = [sources[i] for i in REMOTE]

    def cost(count, extra):
        return pl.CostEstimate(
            flops=4 * frame_count * head_count * count * row_count * row_count * HD,
            transcendentals=frame_count * head_count * count * row_count * row_count,
            bytes_accessed=(2 + 4 * extra + 4) * frame_count * row_count * feature_width,
        )

    stats = pl.pallas_call(
        local_kernel,
        grid_spec=pltpu.PrefetchScalarGridSpec(
            num_scalar_prefetch=1,
            grid=(steps,),
            in_specs=[tile_spec] + [source_spec] * len(local_sources),
            out_specs=[stat_spec, stat_spec, tile_spec],
        ),
        out_shape=[stat_shape, stat_shape, acc_shape],
        cost_estimate=cost(16, len(local_sources)),
    )(flags, queries, *local_sources)
    return pl.pallas_call(
        remote_kernel,
        grid_spec=pltpu.PrefetchScalarGridSpec(
            num_scalar_prefetch=1,
            grid=(steps,),
            in_specs=[tile_spec] + [source_spec] * len(remote_sources)
            + [stat_spec, stat_spec, tile_spec],
            out_specs=tile_spec,
        ),
        out_shape=jax.ShapeDtypeStruct(queries.shape, queries.dtype),
        cost_estimate=cost(10, len(remote_sources)),
    )(flags, queries, *remote_sources, *stats)


def on_device(queries, keys, values, tile_mask):
    stacked = jnp.stack([keys, values], 0)
    sources = fetch_sources(stacked)
    tile_flags = tile_mask[:, 0]
    return attend(queries, sources, tile_flags)


def solution(mesh):
    in_specs = (
        P("tm", "space", None),
        P("tm", "space", None),
        P("tm", "space", None),
        P("tm", "space", None, None),
    )
    out_specs = P("tm", "space", None)
    return jax.shard_map(
        on_device, mesh=mesh, in_specs=in_specs, out_specs=out_specs, check_vma=False
    )
```

```python
import math

import jax
import jax.numpy as jnp
from jax import lax
from jax.experimental import pallas as pl
from jax.experimental.pallas import tpu as pltpu
from jax.sharding import PartitionSpec as P

HD = 128
TR = 2
W = 2


def shifted(block, axis, distance):
    devices = range(lax.axis_size(axis))
    route = [(i - distance, i) for i in devices if i - distance in devices]
    return lax.ppermute(block, axis, route)


def band_list():
    pairs = []
    for d in range(-TR, TR + 1):
        spread = W >> abs(d)
        for e in range(-spread, spread + 1):
            pairs.append((d, e))
    return pairs


def frame_reach(e):
    best = 0
    for d in range(TR + 1):
        if W >> d >= abs(e):
            best = d
    return best


def swap_cores(block):
    devices = range(lax.axis_size("space"))
    return lax.ppermute(block, "space", [(i, i ^ 1) for i in devices])


def fetch_sources(stacked):
    frame_count = stacked.shape[1]
    earlier = shifted(stacked[:, frame_count - TR :], "tm", 1)
    following = shifted(stacked[:, :TR], "tm", -1)
    far_next = shifted(stacked, "space", -2)
    far_prev = shifted(stacked, "space", 2)
    core_zero = lax.axis_index("space") % 2 == 0
    partner_own = swap_cores(stacked)
    partner_far = swap_cores(jnp.where(core_zero, far_next, far_prev))
    near_next = jnp.where(core_zero, partner_own, partner_far)
    near_prev = jnp.where(core_zero, partner_far, partner_own)
    band = jnp.concatenate([earlier[:, TR - 1 :], following[:, :1]], axis=1)
    diag_next = shifted(band, "space", -1)
    diag_prev = shifted(band, "space", 1)
    return (stacked, earlier, following, far_next, far_prev, near_next, near_prev, diag_next, diag_prev)


def locate(frame, d, e):
    offset = frame + d
    if e == 0:
        if offset < 0:
            return 1, offset + TR
        if offset < 2:
            return 0, offset
        return 2, offset - 2
    if abs(e) == 1:
        near, diag = (5, 7) if e > 0 else (6, 8)
        if offset < 0:
            return diag, 0
        if offset < 2:
            return near, offset
        return diag, 1
    return (3 if e > 0 else 4), frame


LOCAL = (0, 3, 4, 5, 6)
HEAD_GROUP = 4
REMOTE = (1, 2, 7, 8)


def scored_pairs(flags_ref, query, sources, frame, kept_sources, lanes):
    score_scale = 1.0 / math.sqrt(HD)
    score_list = []
    value_list = []
    for d, e in band_list():
        which, index = locate(frame, d, e)
        if which not in kept_sources:
            continue
        source = sources[kept_sources.index(which)]
        raw = (
            lax.dot_general(
                query, source[0, index, :, lanes], (((1,), (1,)), ((), ())),
                preferred_element_type=jnp.float32,
            )
            * score_scale
        )
        flag = flags_ref[frame * 25 + (TR + d) * 5 + (W + e)]
        score_list.append(jnp.where(flag > 0, raw, -jnp.inf))
        value_list.append(source[1, index, :, lanes])
    tile_max = score_list[0]
    for scores in score_list[1:]:
        tile_max = jnp.maximum(tile_max, scores)
    return score_list, value_list, jnp.max(tile_max, axis=1, keepdims=True)


def weighted_sums(score_list, value_list, row_max):
    tile_sum = jnp.zeros_like(score_list[0])
    summed = jnp.zeros((row_max.shape[0], HD), jnp.float32)
    for scores, value_tile in zip(score_list, value_list):
        weights = jnp.exp(scores - row_max)
        tile_sum = tile_sum + weights
        summed = summed + jnp.dot(
            weights.astype(jnp.bfloat16), value_tile, preferred_element_type=jnp.float32
        )
    return jnp.sum(tile_sum, axis=1, keepdims=True), summed


def local_kernel(flags_ref, q_ref, *refs):
    *sources, max_ref, sum_ref, acc_ref = refs
    for head in range(max_ref.shape[0]):
        lanes = slice(head * HD, (head + 1) * HD)
        for frame in range(q_ref.shape[0]):
            score_list, value_list, row_max = scored_pairs(
                flags_ref, q_ref[frame, :, lanes], sources, frame, LOCAL, lanes
            )
            denominator, summed = weighted_sums(score_list, value_list, row_max)
            max_ref[head, frame] = row_max
            sum_ref[head, frame] = denominator
            acc_ref[frame, :, lanes] = summed


def remote_kernel(flags_ref, q_ref, *refs):
    *sources, max_ref, sum_ref, acc_ref, o_ref = refs
    for head in range(max_ref.shape[0]):
        lanes = slice(head * HD, (head + 1) * HD)
        for frame in range(q_ref.shape[0]):
            score_list, value_list, remote_max = scored_pairs(
                flags_ref, q_ref[frame, :, lanes], sources, frame, REMOTE, lanes
            )
            local_max = max_ref[head, frame]
            row_max = jnp.maximum(local_max, remote_max)
            rescale = jnp.exp(local_max - row_max)
            denominator, summed = weighted_sums(score_list, value_list, row_max)
            denominator = denominator + rescale * sum_ref[head, frame]
            summed = summed + rescale * acc_ref[frame, :, lanes]
            o_ref[frame, :, lanes] = (summed / denominator).astype(o_ref.dtype)


def attend(queries, sources, tile_flags):
    frame_count, row_count, feature_width = queries.shape
    head_count = feature_width // HD
    group = HEAD_GROUP
    steps = head_count // group
    flags = tile_flags.reshape(-1).astype(jnp.int32)
    source_spec = pl.BlockSpec((2, 2, row_count, group * HD), lambda h, flags: (0, 0, 0, h))
    tile_spec = pl.BlockSpec((frame_count, row_count, group * HD), lambda h, flags: (0, 0, h))
    stat_spec = pl.BlockSpec((group, frame_count, row_count, 1), lambda h, flags: (h, 0, 0, 0))
    stat_shape = jax.ShapeDtypeStruct((head_count, frame_count, row_count, 1), jnp.float32)
    acc_shape = jax.ShapeDtypeStruct(queries.shape, jnp.float32)
    local_sources = [sources[i] for i in LOCAL]
    remote_sources = [sources[i] for i in REMOTE]

    def cost(count, extra):
        return pl.CostEstimate(
            flops=4 * frame_count * head_count * count * row_count * row_count * HD,
            transcendentals=frame_count * head_count * count * row_count * row_count,
            bytes_accessed=(2 + 4 * extra + 4) * frame_count * row_count * feature_width,
        )

    stats = pl.pallas_call(
        local_kernel,
        grid_spec=pltpu.PrefetchScalarGridSpec(
            num_scalar_prefetch=1,
            grid=(steps,),
            in_specs=[tile_spec] + [source_spec] * len(local_sources),
            out_specs=[stat_spec, stat_spec, tile_spec],
        ),
        out_shape=[stat_shape, stat_shape, acc_shape],
        cost_estimate=cost(16, len(local_sources)),
    )(flags, queries, *local_sources)
    return pl.pallas_call(
        remote_kernel,
        grid_spec=pltpu.PrefetchScalarGridSpec(
            num_scalar_prefetch=1,
            grid=(steps,),
            in_specs=[tile_spec] + [source_spec] * len(remote_sources)
            + [stat_spec, stat_spec, tile_spec],
            out_specs=tile_spec,
        ),
        out_shape=jax.ShapeDtypeStruct(queries.shape, queries.dtype),
        cost_estimate=cost(10, len(remote_sources)),
    )(flags, queries, *remote_sources, *stats)


def on_device(queries, keys, values, tile_mask):
    stacked = jnp.stack([keys, values], 0)
    sources = fetch_sources(stacked)
    tile_flags = tile_mask[:, 0]
    return attend(queries, sources, tile_flags)


def solution(mesh):
    in_specs = (
        P("tm", "space", None),
        P("tm", "space", None),
        P("tm", "space", None),
        P("tm", "space", None, None),
    )
    out_specs = P("tm", "space", None)
    return jax.shard_map(
        on_device, mesh=mesh, in_specs=in_specs, out_specs=out_specs, check_vma=False
    )
```

```python
import math

import jax
import jax.numpy as jnp
from jax import lax
from jax.experimental import pallas as pl
from jax.experimental.pallas import tpu as pltpu
from jax.sharding import PartitionSpec as P

HD = 128
TR = 2
W = 2


def shifted(block, axis, distance):
    devices = range(lax.axis_size(axis))
    route = [(i - distance, i) for i in devices if i - distance in devices]
    return lax.ppermute(block, axis, route)


def band_list():
    pairs = []
    for d in range(-TR, TR + 1):
        spread = W >> abs(d)
        for e in range(-spread, spread + 1):
            pairs.append((d, e))
    return pairs


def frame_reach(e):
    best = 0
    for d in range(TR + 1):
        if W >> d >= abs(e):
            best = d
    return best


def swap_cores(block):
    devices = range(lax.axis_size("space"))
    return lax.ppermute(block, "space", [(i, i ^ 1) for i in devices])


def fetch_sources(stacked):
    frame_count = stacked.shape[1]
    earlier = shifted(stacked[:, frame_count - TR :], "tm", 1)
    following = shifted(stacked[:, :TR], "tm", -1)
    far_next = shifted(stacked, "space", -2)
    far_prev = shifted(stacked, "space", 2)
    core_zero = lax.axis_index("space") % 2 == 0
    partner_own = swap_cores(stacked)
    partner_far = swap_cores(jnp.where(core_zero, far_next, far_prev))
    near_next = jnp.where(core_zero, partner_own, partner_far)
    near_prev = jnp.where(core_zero, partner_far, partner_own)
    band = jnp.concatenate([earlier[:, TR - 1 :], following[:, :1]], axis=1)
    diag_next = shifted(band, "space", -1)
    diag_prev = shifted(band, "space", 1)
    return (stacked, earlier, following, far_next, far_prev, near_next, near_prev, diag_next, diag_prev)


def locate(frame, d, e):
    offset = frame + d
    if e == 0:
        if offset < 0:
            return 1, offset + TR
        if offset < 2:
            return 0, offset
        return 2, offset - 2
    if abs(e) == 1:
        near, diag = (5, 7) if e > 0 else (6, 8)
        if offset < 0:
            return diag, 0
        if offset < 2:
            return near, offset
        return diag, 1
    return (3 if e > 0 else 4), frame


LOCAL = (0, 3, 4, 5, 6)
HEAD_GROUP = 4
REMOTE = (1, 2, 7, 8)


def scored_pairs(flags_ref, query, sources, frame, kept_sources, lanes):
    score_scale = 1.0 / math.sqrt(HD)
    score_list = []
    value_list = []
    for d, e in band_list():
        which, index = locate(frame, d, e)
        if which not in kept_sources:
            continue
        source = sources[kept_sources.index(which)]
        raw = (
            lax.dot_general(
                query, source[0, index, :, lanes], (((1,), (1,)), ((), ())),
                preferred_element_type=jnp.float32,
            )
            * score_scale
        )
        flag = flags_ref[frame * 25 + (TR + d) * 5 + (W + e)]
        score_list.append(jnp.where(flag > 0, raw, -jnp.inf))
        value_list.append(source[1, index, :, lanes])
    tile_max = score_list[0]
    for scores in score_list[1:]:
        tile_max = jnp.maximum(tile_max, scores)
    return score_list, value_list, jnp.max(tile_max, axis=1, keepdims=True)


def weighted_sums(score_list, value_list, row_max):
    tile_sum = jnp.zeros_like(score_list[0])
    summed = jnp.zeros((row_max.shape[0], HD), jnp.float32)
    for scores, value_tile in zip(score_list, value_list):
        weights = jnp.exp(scores - row_max)
        tile_sum = tile_sum + weights
        summed = summed + jnp.dot(
            weights.astype(jnp.bfloat16), value_tile, preferred_element_type=jnp.float32
        )
    return jnp.sum(tile_sum, axis=1, keepdims=True), summed


def local_kernel(flags_ref, q_ref, *refs):
    *sources, max_ref, sum_ref, acc_ref = refs

    @pl.loop(0, max_ref.shape[0])
    def _(head):
        lanes = pl.ds(pl.multiple_of(head * HD, HD), HD)
        for frame in range(q_ref.shape[0]):
            score_list, value_list, row_max = scored_pairs(
                flags_ref, q_ref[frame, :, lanes], sources, frame, LOCAL, lanes
            )
            denominator, summed = weighted_sums(score_list, value_list, row_max)
            max_ref[head, frame] = row_max
            sum_ref[head, frame] = denominator
            acc_ref[frame, :, lanes] = summed


def remote_kernel(flags_ref, q_ref, *refs):
    *sources, max_ref, sum_ref, acc_ref, o_ref = refs

    @pl.loop(0, max_ref.shape[0])
    def _(head):
        lanes = pl.ds(pl.multiple_of(head * HD, HD), HD)
        for frame in range(q_ref.shape[0]):
            score_list, value_list, remote_max = scored_pairs(
                flags_ref, q_ref[frame, :, lanes], sources, frame, REMOTE, lanes
            )
            local_max = max_ref[head, frame]
            row_max = jnp.maximum(local_max, remote_max)
            rescale = jnp.exp(local_max - row_max)
            denominator, summed = weighted_sums(score_list, value_list, row_max)
            denominator = denominator + rescale * sum_ref[head, frame]
            summed = summed + rescale * acc_ref[frame, :, lanes]
            o_ref[frame, :, lanes] = (summed / denominator).astype(o_ref.dtype)


def attend(queries, sources, tile_flags):
    frame_count, row_count, feature_width = queries.shape
    head_count = feature_width // HD
    flags = tile_flags.reshape(-1).astype(jnp.int32)
    stat_shape = jax.ShapeDtypeStruct((head_count, frame_count, row_count, 1), jnp.float32)
    acc_shape = jax.ShapeDtypeStruct(queries.shape, jnp.float32)
    local_sources = [sources[i] for i in LOCAL]
    remote_sources = [sources[i] for i in REMOTE]
    smem = pl.BlockSpec(memory_space=pltpu.SMEM)
    vmem = pl.BlockSpec(memory_space=pltpu.VMEM)
    params = pltpu.CompilerParams(vmem_limit_bytes=48 * 1024 * 1024)

    def cost(count, extra):
        return pl.CostEstimate(
            flops=4 * frame_count * head_count * count * row_count * row_count * HD,
            transcendentals=frame_count * head_count * count * row_count * row_count,
            bytes_accessed=(2 + 4 * extra + 4) * frame_count * row_count * feature_width,
        )

    stats = pl.pallas_call(
        local_kernel,
        in_specs=[smem, vmem] + [vmem] * len(local_sources),
        out_specs=[vmem, vmem, vmem],
        out_shape=[stat_shape, stat_shape, acc_shape],
        compiler_params=params,
        cost_estimate=cost(16, len(local_sources)),
    )(flags, queries, *local_sources)
    return pl.pallas_call(
        remote_kernel,
        in_specs=[smem, vmem] + [vmem] * (len(remote_sources) + 3),
        out_specs=vmem,
        out_shape=jax.ShapeDtypeStruct(queries.shape, queries.dtype),
        compiler_params=params,
        cost_estimate=cost(10, len(remote_sources)),
    )(flags, queries, *remote_sources, *stats)


def on_device(queries, keys, values, tile_mask):
    stacked = jnp.stack([keys, values], 0)
    sources = fetch_sources(stacked)
    tile_flags = tile_mask[:, 0]
    return attend(queries, sources, tile_flags)


def solution(mesh):
    in_specs = (
        P("tm", "space", None),
        P("tm", "space", None),
        P("tm", "space", None),
        P("tm", "space", None, None),
    )
    out_specs = P("tm", "space", None)
    return jax.shard_map(
        on_device, mesh=mesh, in_specs=in_specs, out_specs=out_specs, check_vma=False
    )
```

```python
import math

import jax
import jax.numpy as jnp
from jax import lax
from jax.experimental import pallas as pl
from jax.experimental.pallas import tpu as pltpu
from jax.sharding import PartitionSpec as P

HD = 128
TR = 2
W = 2


def shifted(block, axis, distance):
    devices = range(lax.axis_size(axis))
    route = [(i - distance, i) for i in devices if i - distance in devices]
    return lax.ppermute(block, axis, route)


def band_list():
    pairs = []
    for d in range(-TR, TR + 1):
        spread = W >> abs(d)
        for e in range(-spread, spread + 1):
            pairs.append((d, e))
    return pairs


def frame_reach(e):
    best = 0
    for d in range(TR + 1):
        if W >> d >= abs(e):
            best = d
    return best


def swap_cores(block):
    devices = range(lax.axis_size("space"))
    return lax.ppermute(block, "space", [(i, i ^ 1) for i in devices])


def fetch_sources(stacked):
    frame_count = stacked.shape[1]
    earlier = shifted(stacked[:, frame_count - TR :], "tm", 1)
    following = shifted(stacked[:, :TR], "tm", -1)
    far_next = shifted(stacked, "space", -2)
    far_prev = shifted(stacked, "space", 2)
    core_zero = lax.axis_index("space") % 2 == 0
    partner_own = swap_cores(stacked)
    partner_far = swap_cores(jnp.where(core_zero, far_next, far_prev))
    near_next = jnp.where(core_zero, partner_own, partner_far)
    near_prev = jnp.where(core_zero, partner_far, partner_own)
    early_band = earlier[:, TR - 1 :]
    late_band = following[:, :1]
    return (
        stacked, earlier, following, far_next, far_prev, near_next, near_prev,
        shifted(early_band, "space", -1), shifted(early_band, "space", 1),
        shifted(late_band, "space", -1), shifted(late_band, "space", 1),
    )


def locate(frame, d, e):
    offset = frame + d
    if e == 0:
        if offset < 0:
            return 1, offset + TR
        if offset < 2:
            return 0, offset
        return 2, offset - 2
    if abs(e) == 1:
        side = 0 if e > 0 else 1
        if offset < 0:
            return 7 + side, 0
        if offset < 2:
            return 5 + side, offset
        return 9 + side, 0
    return (3 if e > 0 else 4), frame


LOCAL = (0, 3, 4, 5, 6)
HEAD_GROUP = 4
REMOTE = (1, 2, 7, 8, 9, 10)


def scored_pairs(flags_ref, query, sources, frame, kept_sources, lanes):
    score_scale = 1.0 / math.sqrt(HD)
    score_list = []
    value_list = []
    for d, e in band_list():
        which, index = locate(frame, d, e)
        if which not in kept_sources:
            continue
        source = sources[kept_sources.index(which)]
        raw = (
            lax.dot_general(
                query, source[0, index, :, lanes], (((1,), (1,)), ((), ())),
                preferred_element_type=jnp.float32,
            )
            * score_scale
        )
        flag = flags_ref[frame * 25 + (TR + d) * 5 + (W + e)]
        score_list.append(jnp.where(flag > 0, raw, -jnp.inf))
        value_list.append(source[1, index, :, lanes])
    tile_max = score_list[0]
    for scores in score_list[1:]:
        tile_max = jnp.maximum(tile_max, scores)
    return score_list, value_list, jnp.max(tile_max, axis=1, keepdims=True)


def weighted_sums(score_list, value_list, row_max):
    tile_sum = jnp.zeros_like(score_list[0])
    summed = jnp.zeros((row_max.shape[0], HD), jnp.float32)
    for scores, value_tile in zip(score_list, value_list):
        weights = jnp.exp(scores - row_max)
        tile_sum = tile_sum + weights
        summed = summed + jnp.dot(
            weights.astype(jnp.bfloat16), value_tile, preferred_element_type=jnp.float32
        )
    return jnp.sum(tile_sum, axis=1, keepdims=True), summed


def local_kernel(flags_ref, q_ref, *refs):
    *sources, max_ref, sum_ref, acc_ref = refs
    for head in range(max_ref.shape[0]):
        lanes = slice(head * HD, (head + 1) * HD)
        for frame in range(q_ref.shape[0]):
            score_list, value_list, row_max = scored_pairs(
                flags_ref, q_ref[frame, :, lanes], sources, frame, LOCAL, lanes
            )
            denominator, summed = weighted_sums(score_list, value_list, row_max)
            max_ref[head, frame] = row_max
            sum_ref[head, frame] = denominator
            acc_ref[frame, :, lanes] = summed


def remote_kernel(flags_ref, q_ref, *refs):
    *sources, max_ref, sum_ref, acc_ref, o_ref = refs
    for head in range(max_ref.shape[0]):
        lanes = slice(head * HD, (head + 1) * HD)
        for frame in range(q_ref.shape[0]):
            score_list, value_list, remote_max = scored_pairs(
                flags_ref, q_ref[frame, :, lanes], sources, frame, REMOTE, lanes
            )
            local_max = max_ref[head, frame]
            row_max = jnp.maximum(local_max, remote_max)
            rescale = jnp.exp(local_max - row_max)
            denominator, summed = weighted_sums(score_list, value_list, row_max)
            denominator = denominator + rescale * sum_ref[head, frame]
            summed = summed + rescale * acc_ref[frame, :, lanes]
            o_ref[frame, :, lanes] = (summed / denominator).astype(o_ref.dtype)


def attend(queries, sources, tile_flags):
    frame_count, row_count, feature_width = queries.shape
    head_count = feature_width // HD
    group = HEAD_GROUP
    steps = head_count // group
    flags = tile_flags.reshape(-1).astype(jnp.int32)
    def source_spec(source):
        return pl.BlockSpec((2, source.shape[1], row_count, group * HD), lambda h, flags: (0, 0, 0, h))

    tile_spec = pl.BlockSpec((frame_count, row_count, group * HD), lambda h, flags: (0, 0, h))
    stat_spec = pl.BlockSpec((group, frame_count, row_count, 1), lambda h, flags: (h, 0, 0, 0))
    stat_shape = jax.ShapeDtypeStruct((head_count, frame_count, row_count, 1), jnp.float32)
    acc_shape = jax.ShapeDtypeStruct(queries.shape, jnp.float32)
    local_sources = [sources[i] for i in LOCAL]
    remote_sources = [sources[i] for i in REMOTE]

    def cost(count, extra):
        return pl.CostEstimate(
            flops=4 * frame_count * head_count * count * row_count * row_count * HD,
            transcendentals=frame_count * head_count * count * row_count * row_count,
            bytes_accessed=(2 + 4 * extra + 4) * frame_count * row_count * feature_width,
        )

    stats = pl.pallas_call(
        local_kernel,
        grid_spec=pltpu.PrefetchScalarGridSpec(
            num_scalar_prefetch=1,
            grid=(steps,),
            in_specs=[tile_spec] + [source_spec(s) for s in local_sources],
            out_specs=[stat_spec, stat_spec, tile_spec],
        ),
        out_shape=[stat_shape, stat_shape, acc_shape],
        cost_estimate=cost(16, len(local_sources)),
    )(flags, queries, *local_sources)
    return pl.pallas_call(
        remote_kernel,
        grid_spec=pltpu.PrefetchScalarGridSpec(
            num_scalar_prefetch=1,
            grid=(steps,),
            in_specs=[tile_spec] + [source_spec(s) for s in remote_sources]
            + [stat_spec, stat_spec, tile_spec],
            out_specs=tile_spec,
        ),
        out_shape=jax.ShapeDtypeStruct(queries.shape, queries.dtype),
        cost_estimate=cost(10, len(remote_sources)),
    )(flags, queries, *remote_sources, *stats)


def on_device(queries, keys, values, tile_mask):
    stacked = jnp.stack([keys, values], 0)
    sources = fetch_sources(stacked)
    tile_flags = tile_mask[:, 0]
    return attend(queries, sources, tile_flags)


def solution(mesh):
    in_specs = (
        P("tm", "space", None),
        P("tm", "space", None),
        P("tm", "space", None),
        P("tm", "space", None, None),
    )
    out_specs = P("tm", "space", None)
    return jax.shard_map(
        on_device, mesh=mesh, in_specs=in_specs, out_specs=out_specs, check_vma=False
    )
```

```python
import math

import jax
import jax.numpy as jnp
from jax import lax
from jax.experimental import pallas as pl
from jax.experimental.pallas import tpu as pltpu
from jax.sharding import PartitionSpec as P

HD = 128
TR = 2
W = 2


def shifted(block, axis, distance):
    devices = range(lax.axis_size(axis))
    route = [(i - distance, i) for i in devices if i - distance in devices]
    return lax.ppermute(block, axis, route)


def band_list():
    pairs = []
    for d in range(-TR, TR + 1):
        spread = W >> abs(d)
        for e in range(-spread, spread + 1):
            pairs.append((d, e))
    return pairs


def frame_reach(e):
    best = 0
    for d in range(TR + 1):
        if W >> d >= abs(e):
            best = d
    return best


X_CHIPS = 4


def routed(pairs, block):
    return lax.ppermute(block, "tm", pairs) if pairs else jnp.zeros_like(block)


def relayed(block, hops):
    for pairs in hops:
        block = routed(pairs, block)
    return block


def tm_shift(block, step):
    count = lax.axis_size("tm")
    x = X_CHIPS
    if step > 0:
        edge = [t for t in range(count - 1) if t % x == x - 1]
        direct = [(t, t + 1) for t in range(count - 1) if t not in edge]
        via_two = [[(t, t - 1) for t in edge], [(t - 1, t + 3) for t in edge], [(t + 3, t + 1) for t in edge]]
        via_one = [[(t, t - 2) for t in edge], [(t - 2, t + 2) for t in edge], [(t + 2, t + 1) for t in edge]]
    else:
        edge = [t for t in range(1, count) if t % x == 0]
        direct = [(t, t - 1) for t in range(1, count) if t not in edge]
        via_one = [[(t, t + 1) for t in edge], [(t + 1, t - 3) for t in edge], [(t - 3, t - 1) for t in edge]]
        via_two = [[(t, t + 2) for t in edge], [(t + 2, t - 2) for t in edge], [(t - 2, t - 1) for t in edge]]
    plain = routed(direct, block)
    keys_part = relayed(block[:1], via_one)
    values_part = relayed(block[1:], via_two)
    position = lax.axis_index("tm") % x
    at_edge = position == (0 if step > 0 else x - 1)
    return jnp.where(at_edge, jnp.concatenate([keys_part, values_part], axis=0), plain)


def swap_cores(block):
    devices = range(lax.axis_size("space"))
    return lax.ppermute(block, "space", [(i, i ^ 1) for i in devices])


def fetch_sources(stacked):
    frame_count = stacked.shape[1]
    earlier = tm_shift(stacked[:, frame_count - TR :], 1)
    following = tm_shift(stacked[:, :TR], -1)
    far_next = shifted(stacked, "space", -2)
    far_prev = shifted(stacked, "space", 2)
    core_zero = lax.axis_index("space") % 2 == 0
    partner_own = swap_cores(stacked)
    partner_far = swap_cores(jnp.where(core_zero, far_next, far_prev))
    near_next = jnp.where(core_zero, partner_own, partner_far)
    near_prev = jnp.where(core_zero, partner_far, partner_own)
    early_band = earlier[:, TR - 1 :]
    late_band = following[:, :1]
    return (
        stacked, earlier, following, far_next, far_prev, near_next, near_prev,
        shifted(early_band, "space", -1), shifted(early_band, "space", 1),
        shifted(late_band, "space", -1), shifted(late_band, "space", 1),
    )


def locate(frame, d, e):
    offset = frame + d
    if e == 0:
        if offset < 0:
            return 1, offset + TR
        if offset < 2:
            return 0, offset
        return 2, offset - 2
    if abs(e) == 1:
        side = 0 if e > 0 else 1
        if offset < 0:
            return 7 + side, 0
        if offset < 2:
            return 5 + side, offset
        return 9 + side, 0
    return (3 if e > 0 else 4), frame


LOCAL = (0, 3, 4, 5, 6)
HEAD_GROUP = 4
REMOTE = (1, 2, 7, 8, 9, 10)


def scored_pairs(flags_ref, query, sources, frame, kept_sources, lanes):
    score_scale = 1.0 / math.sqrt(HD)
    score_list = []
    value_list = []
    for d, e in band_list():
        which, index = locate(frame, d, e)
        if which not in kept_sources:
            continue
        source = sources[kept_sources.index(which)]
        raw = (
            lax.dot_general(
                query, source[0, index, :, lanes], (((1,), (1,)), ((), ())),
                preferred_element_type=jnp.float32,
            )
            * score_scale
        )
        flag = flags_ref[frame * 25 + (TR + d) * 5 + (W + e)]
        score_list.append(jnp.where(flag > 0, raw, -jnp.inf))
        value_list.append(source[1, index, :, lanes])
    tile_max = score_list[0]
    for scores in score_list[1:]:
        tile_max = jnp.maximum(tile_max, scores)
    return score_list, value_list, jnp.max(tile_max, axis=1, keepdims=True)


def weighted_sums(score_list, value_list, row_max):
    tile_sum = jnp.zeros_like(score_list[0])
    summed = jnp.zeros((row_max.shape[0], HD), jnp.float32)
    for scores, value_tile in zip(score_list, value_list):
        weights = jnp.exp(scores - row_max)
        tile_sum = tile_sum + weights
        summed = summed + jnp.dot(
            weights.astype(jnp.bfloat16), value_tile, preferred_element_type=jnp.float32
        )
    return jnp.sum(tile_sum, axis=1, keepdims=True), summed


def local_kernel(flags_ref, q_ref, *refs):
    *sources, max_ref, sum_ref, acc_ref = refs
    for head in range(max_ref.shape[0]):
        lanes = slice(head * HD, (head + 1) * HD)
        for frame in range(q_ref.shape[0]):
            score_list, value_list, row_max = scored_pairs(
                flags_ref, q_ref[frame, :, lanes], sources, frame, LOCAL, lanes
            )
            denominator, summed = weighted_sums(score_list, value_list, row_max)
            max_ref[head, frame] = row_max
            sum_ref[head, frame] = denominator
            acc_ref[frame, :, lanes] = summed


def remote_kernel(flags_ref, q_ref, *refs):
    *sources, max_ref, sum_ref, acc_ref, o_ref = refs
    for head in range(max_ref.shape[0]):
        lanes = slice(head * HD, (head + 1) * HD)
        for frame in range(q_ref.shape[0]):
            score_list, value_list, remote_max = scored_pairs(
                flags_ref, q_ref[frame, :, lanes], sources, frame, REMOTE, lanes
            )
            local_max = max_ref[head, frame]
            row_max = jnp.maximum(local_max, remote_max)
            rescale = jnp.exp(local_max - row_max)
            denominator, summed = weighted_sums(score_list, value_list, row_max)
            denominator = denominator + rescale * sum_ref[head, frame]
            summed = summed + rescale * acc_ref[frame, :, lanes]
            o_ref[frame, :, lanes] = (summed / denominator).astype(o_ref.dtype)


def attend(queries, sources, tile_flags):
    frame_count, row_count, feature_width = queries.shape
    head_count = feature_width // HD
    group = HEAD_GROUP
    steps = head_count // group
    flags = tile_flags.reshape(-1).astype(jnp.int32)
    def source_spec(source):
        return pl.BlockSpec((2, source.shape[1], row_count, group * HD), lambda h, flags: (0, 0, 0, h))

    tile_spec = pl.BlockSpec((frame_count, row_count, group * HD), lambda h, flags: (0, 0, h))
    stat_spec = pl.BlockSpec((group, frame_count, row_count, 1), lambda h, flags: (h, 0, 0, 0))
    stat_shape = jax.ShapeDtypeStruct((head_count, frame_count, row_count, 1), jnp.float32)
    acc_shape = jax.ShapeDtypeStruct(queries.shape, jnp.float32)
    local_sources = [sources[i] for i in LOCAL]
    remote_sources = [sources[i] for i in REMOTE]

    def cost(count, extra):
        return pl.CostEstimate(
            flops=4 * frame_count * head_count * count * row_count * row_count * HD,
            transcendentals=frame_count * head_count * count * row_count * row_count,
            bytes_accessed=(2 + 4 * extra + 4) * frame_count * row_count * feature_width,
        )

    stats = pl.pallas_call(
        local_kernel,
        grid_spec=pltpu.PrefetchScalarGridSpec(
            num_scalar_prefetch=1,
            grid=(steps,),
            in_specs=[tile_spec] + [source_spec(s) for s in local_sources],
            out_specs=[stat_spec, stat_spec, tile_spec],
        ),
        out_shape=[stat_shape, stat_shape, acc_shape],
        cost_estimate=cost(16, len(local_sources)),
    )(flags, queries, *local_sources)
    return pl.pallas_call(
        remote_kernel,
        grid_spec=pltpu.PrefetchScalarGridSpec(
            num_scalar_prefetch=1,
            grid=(steps,),
            in_specs=[tile_spec] + [source_spec(s) for s in remote_sources]
            + [stat_spec, stat_spec, tile_spec],
            out_specs=tile_spec,
        ),
        out_shape=jax.ShapeDtypeStruct(queries.shape, queries.dtype),
        cost_estimate=cost(10, len(remote_sources)),
    )(flags, queries, *remote_sources, *stats)


def on_device(queries, keys, values, tile_mask):
    stacked = jnp.stack([keys, values], 0)
    sources = fetch_sources(stacked)
    tile_flags = tile_mask[:, 0]
    return attend(queries, sources, tile_flags)


def solution(mesh):
    in_specs = (
        P("tm", "space", None),
        P("tm", "space", None),
        P("tm", "space", None),
        P("tm", "space", None, None),
    )
    out_specs = P("tm", "space", None)
    return jax.shard_map(
        on_device, mesh=mesh, in_specs=in_specs, out_specs=out_specs, check_vma=False
    )
```

```python
import math

import jax
import jax.numpy as jnp
from jax import lax
from jax.experimental import pallas as pl
from jax.experimental.pallas import tpu as pltpu
from jax.sharding import PartitionSpec as P


HD = 128
TR = 2
W = 2


def shifted(block, axis, distance):
    devices = range(lax.axis_size(axis))
    route = [(i - distance, i) for i in devices if i - distance in devices]
    return lax.ppermute(block, axis, route)


def band_list():
    pairs = []
    for d in range(-TR, TR + 1):
        spread = W >> abs(d)
        for e in range(-spread, spread + 1):
            pairs.append((d, e))
    return pairs


X_CHIPS = 4


def routed(pairs, block):
    return lax.ppermute(block, "tm", pairs) if pairs else jnp.zeros_like(block)


def relayed(block, hops):
    for pairs in hops:
        block = routed(pairs, block)
    return block


def tm_shift(block, step):
    count = lax.axis_size("tm")
    x = X_CHIPS
    if step > 0:
        edge = [t for t in range(count - 1) if t % x == x - 1]
        direct = [(t, t + 1) for t in range(count - 1) if t not in edge]
        via_two = [[(t, t - 1) for t in edge], [(t - 1, t + 3) for t in edge], [(t + 3, t + 1) for t in edge]]
        via_one = [[(t, t - 2) for t in edge], [(t - 2, t + 2) for t in edge], [(t + 2, t + 1) for t in edge]]
    else:
        edge = [t for t in range(1, count) if t % x == 0]
        direct = [(t, t - 1) for t in range(1, count) if t not in edge]
        via_one = [[(t, t + 1) for t in edge], [(t + 1, t - 3) for t in edge], [(t - 3, t - 1) for t in edge]]
        via_two = [[(t, t + 2) for t in edge], [(t + 2, t - 2) for t in edge], [(t - 2, t - 1) for t in edge]]
    plain = routed(direct, block)
    keys_part = relayed(block[:1], via_one)
    values_part = relayed(block[1:], via_two)
    position = lax.axis_index("tm") % x
    at_edge = position == (0 if step > 0 else x - 1)
    return jnp.where(at_edge, jnp.concatenate([keys_part, values_part], axis=0), plain)


def swap_cores(block):
    devices = range(lax.axis_size("space"))
    return lax.ppermute(block, "space", [(i, i ^ 1) for i in devices])


def fetch_sources(stacked):
    frame_count = stacked.shape[1]
    earlier = tm_shift(stacked[:, frame_count - TR :], 1)
    following = tm_shift(stacked[:, :TR], -1)
    far_next = shifted(stacked, "space", -2)
    far_prev = shifted(stacked, "space", 2)
    core_zero = lax.axis_index("space") % 2 == 0
    partner_own = swap_cores(stacked)
    partner_far = swap_cores(jnp.where(core_zero, far_next, far_prev))
    near_next = jnp.where(core_zero, partner_own, partner_far)
    near_prev = jnp.where(core_zero, partner_far, partner_own)
    early_band = earlier[:, TR - 1 :]
    late_band = following[:, :1]
    return (
        stacked, earlier, following, far_next, far_prev, near_next, near_prev,
        shifted(early_band, "space", -1), shifted(early_band, "space", 1),
        shifted(late_band, "space", -1), shifted(late_band, "space", 1),
    )


def locate(frame, d, e):
    offset = frame + d
    if e == 0:
        if offset < 0:
            return 1, offset + TR
        if offset < 2:
            return 0, offset
        return 2, offset - 2
    if abs(e) == 1:
        side = 0 if e > 0 else 1
        if offset < 0:
            return 7 + side, 0
        if offset < 2:
            return 5 + side, offset
        return 9 + side, 0
    return (3 if e > 0 else 4), frame


LOCAL = (0, 3, 4, 5, 6)
HEAD_GROUP = 4
REMOTE = (1, 2, 7, 8, 9, 10)


def scored_pairs(flags_ref, query, sources, frame, kept_sources, lanes):
    score_scale = 1.0 / math.sqrt(HD)
    score_list = []
    value_list = []
    for d, e in band_list():
        which, index = locate(frame, d, e)
        if which not in kept_sources:
            continue
        source = sources[kept_sources.index(which)]
        raw = (
            lax.dot_general(
                query, source[0, index, :, lanes], (((1,), (1,)), ((), ())),
                preferred_element_type=jnp.float32,
            )
            * score_scale
        )
        flag = flags_ref[frame * 25 + (TR + d) * 5 + (W + e)]
        score_list.append(jnp.where(flag > 0, raw, -jnp.inf))
        value_list.append(source[1, index, :, lanes])
    tile_max = score_list[0]
    for scores in score_list[1:]:
        tile_max = jnp.maximum(tile_max, scores)
    return score_list, value_list, jnp.max(tile_max, axis=1, keepdims=True)


def weighted_sums(score_list, value_list, row_max):
    tile_sum = jnp.zeros_like(score_list[0])
    summed = jnp.zeros((row_max.shape[0], HD), jnp.float32)
    for scores, value_tile in zip(score_list, value_list):
        weights = jnp.exp(scores - row_max)
        tile_sum = tile_sum + weights
        summed = summed + jnp.dot(
            weights.astype(jnp.bfloat16), value_tile, preferred_element_type=jnp.float32
        )
    return jnp.sum(tile_sum, axis=1, keepdims=True), summed


def local_kernel(flags_ref, q_ref, *refs):
    *sources, max_ref, sum_ref, acc_ref = refs
    for head in range(max_ref.shape[0]):
        lanes = slice(head * HD, (head + 1) * HD)
        for frame in range(q_ref.shape[0]):
            score_list, value_list, row_max = scored_pairs(
                flags_ref, q_ref[frame, :, lanes], sources, frame, LOCAL, lanes
            )
            denominator, summed = weighted_sums(score_list, value_list, row_max)
            max_ref[head, frame] = row_max
            sum_ref[head, frame] = denominator
            acc_ref[frame, :, lanes] = summed


def remote_kernel(flags_ref, q_ref, *refs):
    *sources, max_ref, sum_ref, acc_ref, o_ref = refs
    for head in range(max_ref.shape[0]):
        lanes = slice(head * HD, (head + 1) * HD)
        for frame in range(q_ref.shape[0]):
            score_list, value_list, remote_max = scored_pairs(
                flags_ref, q_ref[frame, :, lanes], sources, frame, REMOTE, lanes
            )
            local_max = max_ref[head, frame]
            row_max = jnp.maximum(local_max, remote_max)
            rescale = jnp.exp(local_max - row_max)
            denominator, summed = weighted_sums(score_list, value_list, row_max)
            denominator = denominator + rescale * sum_ref[head, frame]
            summed = summed + rescale * acc_ref[frame, :, lanes]
            o_ref[frame, :, lanes] = (summed / denominator).astype(o_ref.dtype)


def attend(queries, sources, tile_flags):
    frame_count, row_count, feature_width = queries.shape
    head_count = feature_width // HD
    group = HEAD_GROUP
    steps = head_count // group
    flags = tile_flags.reshape(-1).astype(jnp.int32)

    def source_spec(source):
        return pl.BlockSpec((2, source.shape[1], row_count, group * HD), lambda h, flags: (0, 0, 0, h))

    tile_spec = pl.BlockSpec((frame_count, row_count, group * HD), lambda h, flags: (0, 0, h))
    stat_spec = pl.BlockSpec((group, frame_count, row_count, 1), lambda h, flags: (h, 0, 0, 0))
    stat_shape = jax.ShapeDtypeStruct((head_count, frame_count, row_count, 1), jnp.float32)
    acc_shape = jax.ShapeDtypeStruct(queries.shape, jnp.float32)
    local_sources = [sources[i] for i in LOCAL]
    remote_sources = [sources[i] for i in REMOTE]

    def cost(count, extra):
        return pl.CostEstimate(
            flops=4 * frame_count * head_count * count * row_count * row_count * HD,
            transcendentals=frame_count * head_count * count * row_count * row_count,
            bytes_accessed=(2 + 4 * extra + 4) * frame_count * row_count * feature_width,
        )

    local_call = pl.pallas_call(
        local_kernel,
        grid_spec=pltpu.PrefetchScalarGridSpec(
            num_scalar_prefetch=1,
            grid=(steps,),
            in_specs=[tile_spec] + [source_spec(s) for s in local_sources],
            out_specs=[stat_spec, stat_spec, tile_spec],
        ),
        out_shape=[stat_shape, stat_shape, acc_shape],
        cost_estimate=cost(16, len(local_sources)),
    )
    stats = local_call(flags, queries, *local_sources)
    return pl.pallas_call(
        remote_kernel,
        grid_spec=pltpu.PrefetchScalarGridSpec(
            num_scalar_prefetch=1,
            grid=(steps,),
            in_specs=[tile_spec] + [source_spec(s) for s in remote_sources]
            + [stat_spec, stat_spec, tile_spec],
            out_specs=tile_spec,
        ),
        out_shape=jax.ShapeDtypeStruct(queries.shape, queries.dtype),
        cost_estimate=cost(10, len(remote_sources)),
    )(flags, queries, *remote_sources, *stats)


def on_device(queries, keys, values, tile_mask):
    stacked = jnp.stack([keys, values], 0)
    sources = fetch_sources(stacked)
    tile_flags = tile_mask[:, 0]
    return attend(queries, sources, tile_flags)


def solution(mesh):
    in_specs = (
        P("tm", "space", None),
        P("tm", "space", None),
        P("tm", "space", None),
        P("tm", "space", None, None),
    )
    out_specs = P("tm", "space", None)
    return jax.shard_map(
        on_device, mesh=mesh, in_specs=in_specs, out_specs=out_specs, check_vma=False
    )
```

```python
import math

import jax
import jax.numpy as jnp
from jax import lax
from jax.experimental import pallas as pl
from jax.experimental.pallas import tpu as pltpu
from jax.sharding import PartitionSpec as P

HD = 128
TR = 2
W = 2


def shifted(block, axis, distance):
    devices = range(lax.axis_size(axis))
    route = [(i - distance, i) for i in devices if i - distance in devices]
    return lax.ppermute(block, axis, route)


def band_list():
    pairs = []
    for d in range(-TR, TR + 1):
        spread = W >> abs(d)
        for e in range(-spread, spread + 1):
            pairs.append((d, e))
    return pairs


def frame_reach(e):
    best = 0
    for d in range(TR + 1):
        if W >> d >= abs(e):
            best = d
    return best


X_CHIPS = 4


def routed(pairs, block):
    return lax.ppermute(block, "tm", pairs) if pairs else jnp.zeros_like(block)


def relayed(block, hops):
    for pairs in hops:
        block = routed(pairs, block)
    return block


def tm_shift(block, step):
    count = lax.axis_size("tm")
    x = X_CHIPS
    if step > 0:
        edge = [t for t in range(count - 1) if t % x == x - 1]
        direct = [(t, t + 1) for t in range(count - 1) if t not in edge]
        via_two = [[(t, t - 1) for t in edge], [(t - 1, t + 3) for t in edge], [(t + 3, t + 1) for t in edge]]
        via_one = [[(t, t - 2) for t in edge], [(t - 2, t + 2) for t in edge], [(t + 2, t + 1) for t in edge]]
    else:
        edge = [t for t in range(1, count) if t % x == 0]
        direct = [(t, t - 1) for t in range(1, count) if t not in edge]
        via_one = [[(t, t + 1) for t in edge], [(t + 1, t - 3) for t in edge], [(t - 3, t - 1) for t in edge]]
        via_two = [[(t, t + 2) for t in edge], [(t + 2, t - 2) for t in edge], [(t - 2, t - 1) for t in edge]]
    plain = routed(direct, block)
    keys_part = relayed(block[:1], via_one)
    values_part = relayed(block[1:], via_two)
    position = lax.axis_index("tm") % x
    at_edge = position == (0 if step > 0 else x - 1)
    return jnp.where(at_edge, jnp.concatenate([keys_part, values_part], axis=0), plain)


def swap_cores(block):
    devices = range(lax.axis_size("space"))
    return lax.ppermute(block, "space", [(i, i ^ 1) for i in devices])


def fetch_sources(stacked):
    frame_count = stacked.shape[1]
    earlier = tm_shift(stacked[:, frame_count - TR :], 1)
    following = tm_shift(stacked[:, :TR], -1)
    far_next = shifted(stacked, "space", -2)
    far_prev = shifted(stacked, "space", 2)
    core_zero = lax.axis_index("space") % 2 == 0
    partner_own = swap_cores(stacked)
    partner_far = swap_cores(jnp.where(core_zero, far_next, far_prev))
    near_next = jnp.where(core_zero, partner_own, partner_far)
    near_prev = jnp.where(core_zero, partner_far, partner_own)
    early_band = earlier[:, TR - 1 :]
    late_band = following[:, :1]
    return (
        stacked, earlier, following, far_next, far_prev, near_next, near_prev,
        shifted(early_band, "space", -1), shifted(early_band, "space", 1),
        shifted(late_band, "space", -1), shifted(late_band, "space", 1),
    )


def locate(frame, d, e):
    offset = frame + d
    if e == 0:
        if offset < 0:
            return 1, offset + TR
        if offset < 2:
            return 0, offset
        return 2, offset - 2
    if abs(e) == 1:
        side = 0 if e > 0 else 1
        if offset < 0:
            return 7 + side, 0
        if offset < 2:
            return 5 + side, offset
        return 9 + side, 0
    return (3 if e > 0 else 4), frame


LOCAL = (0, 3, 4, 5, 6)
HEAD_GROUP = 4
REMOTE = (1, 2, 7, 8, 9, 10)


def scored_pairs(flags_ref, query, sources, frame, kept_sources, lanes):
    score_scale = 1.0 / math.sqrt(HD)
    score_list = []
    value_list = []
    for d, e in band_list():
        which, index = locate(frame, d, e)
        if which not in kept_sources:
            continue
        source = sources[kept_sources.index(which)]
        raw = (
            lax.dot_general(
                query, source[0, index, :, lanes], (((1,), (1,)), ((), ())),
                preferred_element_type=jnp.float32,
            )
            * score_scale
        )
        flag = flags_ref[frame * 25 + (TR + d) * 5 + (W + e)]
        score_list.append(jnp.where(flag > 0, raw, -jnp.inf))
        value_list.append(source[1, index, :, lanes])
    tile_max = score_list[0]
    for scores in score_list[1:]:
        tile_max = jnp.maximum(tile_max, scores)
    return score_list, value_list, jnp.max(tile_max, axis=1, keepdims=True)


def weighted_sums(score_list, value_list, row_max):
    tile_sum = jnp.zeros_like(score_list[0])
    summed = jnp.zeros((row_max.shape[0], HD), jnp.float32)
    for scores, value_tile in zip(score_list, value_list):
        weights = jnp.exp(scores - row_max)
        tile_sum = tile_sum + weights
        summed = summed + jnp.dot(
            weights.astype(jnp.bfloat16), value_tile, preferred_element_type=jnp.float32
        )
    return jnp.sum(tile_sum, axis=1, keepdims=True), summed


def attention_kernel(flags_ref, q_ref, *refs):
    *sources, o_ref = refs
    everything = tuple(range(len(sources)))
    for head in range(HEAD_GROUP):
        lanes = slice(head * HD, (head + 1) * HD)
        for frame in range(q_ref.shape[0]):
            score_list, value_list, row_max = scored_pairs(
                flags_ref, q_ref[frame, :, lanes], sources, frame, everything, lanes
            )
            denominator, summed = weighted_sums(score_list, value_list, row_max)
            o_ref[frame, :, lanes] = (summed / denominator).astype(o_ref.dtype)


def attend(queries, sources, tile_flags):
    frame_count, row_count, feature_width = queries.shape
    head_count = feature_width // HD
    steps = head_count // HEAD_GROUP
    flags = tile_flags.reshape(-1).astype(jnp.int32)
    tile_spec = pl.BlockSpec(
        (frame_count, row_count, HEAD_GROUP * HD), lambda h, flags: (0, 0, h)
    )

    def source_spec(source):
        return pl.BlockSpec(
            (2, source.shape[1], row_count, HEAD_GROUP * HD), lambda h, flags: (0, 0, 0, h)
        )

    pairs = len(band_list())
    cost = pl.CostEstimate(
        flops=4 * frame_count * head_count * pairs * row_count * row_count * HD,
        transcendentals=frame_count * head_count * pairs * row_count * row_count,
        bytes_accessed=(2 + 4 * len(sources)) * frame_count * row_count * feature_width,
    )
    return pl.pallas_call(
        attention_kernel,
        grid_spec=pltpu.PrefetchScalarGridSpec(
            num_scalar_prefetch=1,
            grid=(steps,),
            in_specs=[tile_spec] + [source_spec(s) for s in sources],
            out_specs=tile_spec,
        ),
        out_shape=jax.ShapeDtypeStruct(queries.shape, queries.dtype),
        cost_estimate=cost,
    )(flags, queries, *sources)


def on_device(queries, keys, values, tile_mask):
    stacked = jnp.stack([keys, values], 0)
    sources = fetch_sources(stacked)
    tile_flags = tile_mask[:, 0]
    return attend(queries, sources, tile_flags)


def solution(mesh):
    in_specs = (
        P("tm", "space", None),
        P("tm", "space", None),
        P("tm", "space", None),
        P("tm", "space", None, None),
    )
    out_specs = P("tm", "space", None)
    return jax.shard_map(
        on_device, mesh=mesh, in_specs=in_specs, out_specs=out_specs, check_vma=False
    )
```

```python
import math

import jax
import jax.numpy as jnp
from jax import lax
from jax.experimental import pallas as pl
from jax.experimental.pallas import tpu as pltpu
from jax.sharding import PartitionSpec as P

HD = 128
TR = 2
W = 2


def shifted(block, axis, distance):
    devices = range(lax.axis_size(axis))
    route = [(i - distance, i) for i in devices if i - distance in devices]
    return lax.ppermute(block, axis, route)


def band_list():
    pairs = []
    for d in range(-TR, TR + 1):
        spread = W >> abs(d)
        for e in range(-spread, spread + 1):
            pairs.append((d, e))
    return pairs


def frame_reach(e):
    best = 0
    for d in range(TR + 1):
        if W >> d >= abs(e):
            best = d
    return best


X_CHIPS = 4


def routed(pairs, block):
    return lax.ppermute(block, "tm", pairs) if pairs else jnp.zeros_like(block)


def relayed(block, hops):
    for pairs in hops:
        block = routed(pairs, block)
    return block


def tm_shift(block, step):
    count = lax.axis_size("tm")
    x = X_CHIPS
    if step > 0:
        edge = [t for t in range(count - 1) if t % x == x - 1]
        direct = [(t, t + 1) for t in range(count - 1) if t not in edge]
        via_two = [[(t, t - 1) for t in edge], [(t - 1, t + 3) for t in edge], [(t + 3, t + 1) for t in edge]]
        via_one = [[(t, t - 2) for t in edge], [(t - 2, t + 2) for t in edge], [(t + 2, t + 1) for t in edge]]
    else:
        edge = [t for t in range(1, count) if t % x == 0]
        direct = [(t, t - 1) for t in range(1, count) if t not in edge]
        via_one = [[(t, t + 1) for t in edge], [(t + 1, t - 3) for t in edge], [(t - 3, t - 1) for t in edge]]
        via_two = [[(t, t + 2) for t in edge], [(t + 2, t - 2) for t in edge], [(t - 2, t - 1) for t in edge]]
    plain = routed(direct, block)
    keys_part = relayed(block[:1], via_one)
    values_part = relayed(block[1:], via_two)
    position = lax.axis_index("tm") % x
    at_edge = position == (0 if step > 0 else x - 1)
    return jnp.where(at_edge, jnp.concatenate([keys_part, values_part], axis=0), plain)


def swap_cores(block):
    devices = range(lax.axis_size("space"))
    return lax.ppermute(block, "space", [(i, i ^ 1) for i in devices])


def fetch_sources(stacked):
    frame_count = stacked.shape[1]
    earlier = tm_shift(stacked[:, frame_count - TR :], 1)
    following = tm_shift(stacked[:, :TR], -1)
    far_next = shifted(stacked, "space", -2)
    far_prev = shifted(stacked, "space", 2)
    core_zero = lax.axis_index("space") % 2 == 0
    partner_own = swap_cores(stacked)
    partner_far = swap_cores(jnp.where(core_zero, far_next, far_prev))
    near_next = jnp.where(core_zero, partner_own, partner_far)
    near_prev = jnp.where(core_zero, partner_far, partner_own)
    early_band = earlier[:, TR - 1 :]
    late_band = following[:, :1]
    return (
        stacked, earlier, following, far_next, far_prev, near_next, near_prev,
        shifted(early_band, "space", -1), shifted(early_band, "space", 1),
        shifted(late_band, "space", -1), shifted(late_band, "space", 1),
    )


def locate(frame, d, e):
    offset = frame + d
    if e == 0:
        if offset < 0:
            return 1, offset + TR
        if offset < 2:
            return 0, offset
        return 2, offset - 2
    if abs(e) == 1:
        side = 0 if e > 0 else 1
        if offset < 0:
            return 7 + side, 0
        if offset < 2:
            return 5 + side, offset
        return 9 + side, 0
    return (3 if e > 0 else 4), frame


LOCAL = (0, 3, 4, 5, 6)
HEAD_GROUP = 6
REMOTE = (1, 2, 7, 8, 9, 10)


def scored_pairs(flags_ref, query, sources, frame, kept_sources, lanes):
    score_scale = 1.0 / math.sqrt(HD)
    score_list = []
    value_list = []
    for d, e in band_list():
        which, index = locate(frame, d, e)
        if which not in kept_sources:
            continue
        source = sources[kept_sources.index(which)]
        raw = (
            lax.dot_general(
                query, source[0, index, :, lanes], (((1,), (1,)), ((), ())),
                preferred_element_type=jnp.float32,
            )
            * score_scale
        )
        flag = flags_ref[frame * 25 + (TR + d) * 5 + (W + e)]
        score_list.append(jnp.where(flag > 0, raw, -jnp.inf))
        value_list.append(source[1, index, :, lanes])
    tile_max = score_list[0]
    for scores in score_list[1:]:
        tile_max = jnp.maximum(tile_max, scores)
    return score_list, value_list, jnp.max(tile_max, axis=1, keepdims=True)


def weighted_sums(score_list, value_list, row_max):
    tile_sum = jnp.zeros_like(score_list[0])
    summed = jnp.zeros((row_max.shape[0], HD), jnp.float32)
    for scores, value_tile in zip(score_list, value_list):
        weights = jnp.exp(scores - row_max)
        tile_sum = tile_sum + weights
        summed = summed + jnp.dot(
            weights.astype(jnp.bfloat16), value_tile, preferred_element_type=jnp.float32
        )
    return jnp.sum(tile_sum, axis=1, keepdims=True), summed


def attention_kernel(flags_ref, q_ref, *refs):
    *sources, o_ref = refs
    everything = tuple(range(len(sources)))
    for head in range(HEAD_GROUP):
        lanes = slice(head * HD, (head + 1) * HD)
        for frame in range(q_ref.shape[0]):
            score_list, value_list, row_max = scored_pairs(
                flags_ref, q_ref[frame, :, lanes], sources, frame, everything, lanes
            )
            denominator, summed = weighted_sums(score_list, value_list, row_max)
            o_ref[frame, :, lanes] = (summed / denominator).astype(o_ref.dtype)


def attend(queries, sources, tile_flags):
    frame_count, row_count, feature_width = queries.shape
    head_count = feature_width // HD
    steps = head_count // HEAD_GROUP
    flags = tile_flags.reshape(-1).astype(jnp.int32)
    tile_spec = pl.BlockSpec(
        (frame_count, row_count, HEAD_GROUP * HD), lambda h, flags: (0, 0, h)
    )

    def source_spec(source):
        return pl.BlockSpec(
            (2, source.shape[1], row_count, HEAD_GROUP * HD), lambda h, flags: (0, 0, 0, h)
        )

    pairs = len(band_list())
    cost = pl.CostEstimate(
        flops=4 * frame_count * head_count * pairs * row_count * row_count * HD,
        transcendentals=frame_count * head_count * pairs * row_count * row_count,
        bytes_accessed=(2 + 4 * len(sources)) * frame_count * row_count * feature_width,
    )
    return pl.pallas_call(
        attention_kernel,
        grid_spec=pltpu.PrefetchScalarGridSpec(
            num_scalar_prefetch=1,
            grid=(steps,),
            in_specs=[tile_spec] + [source_spec(s) for s in sources],
            out_specs=tile_spec,
        ),
        out_shape=jax.ShapeDtypeStruct(queries.shape, queries.dtype),
        cost_estimate=cost,
    )(flags, queries, *sources)


def on_device(queries, keys, values, tile_mask):
    stacked = jnp.stack([keys, values], 0)
    sources = fetch_sources(stacked)
    tile_flags = tile_mask[:, 0]
    return attend(queries, sources, tile_flags)


def solution(mesh):
    in_specs = (
        P("tm", "space", None),
        P("tm", "space", None),
        P("tm", "space", None),
        P("tm", "space", None, None),
    )
    out_specs = P("tm", "space", None)
    return jax.shard_map(
        on_device, mesh=mesh, in_specs=in_specs, out_specs=out_specs, check_vma=False
    )
```

```python
import math

import jax
import jax.numpy as jnp
from jax import lax
from jax.experimental import pallas as pl
from jax.experimental.pallas import tpu as pltpu
from jax.sharding import PartitionSpec as P

HD = 128
TR = 2
W = 2


def shifted(block, axis, distance):
    devices = range(lax.axis_size(axis))
    route = [(i - distance, i) for i in devices if i - distance in devices]
    return lax.ppermute(block, axis, route)


def band_list():
    pairs = []
    for d in range(-TR, TR + 1):
        spread = W >> abs(d)
        for e in range(-spread, spread + 1):
            pairs.append((d, e))
    return pairs


def frame_reach(e):
    best = 0
    for d in range(TR + 1):
        if W >> d >= abs(e):
            best = d
    return best


X_CHIPS = 4


def routed(pairs, block):
    return lax.ppermute(block, "tm", pairs) if pairs else jnp.zeros_like(block)


def relayed(block, hops):
    for pairs in hops:
        block = routed(pairs, block)
    return block


def tm_shift(block, step):
    count = lax.axis_size("tm")
    x = X_CHIPS
    if step > 0:
        edge = [t for t in range(count - 1) if t % x == x - 1]
        direct = [(t, t + 1) for t in range(count - 1) if t not in edge]
        via_two = [[(t, t - 1) for t in edge], [(t - 1, t + 3) for t in edge], [(t + 3, t + 1) for t in edge]]
        via_one = [[(t, t - 2) for t in edge], [(t - 2, t + 2) for t in edge], [(t + 2, t + 1) for t in edge]]
    else:
        edge = [t for t in range(1, count) if t % x == 0]
        direct = [(t, t - 1) for t in range(1, count) if t not in edge]
        via_one = [[(t, t + 1) for t in edge], [(t + 1, t - 3) for t in edge], [(t - 3, t - 1) for t in edge]]
        via_two = [[(t, t + 2) for t in edge], [(t + 2, t - 2) for t in edge], [(t - 2, t - 1) for t in edge]]
    plain = routed(direct, block)
    keys_part = relayed(block[:1], via_one)
    values_part = relayed(block[1:], via_two)
    position = lax.axis_index("tm") % x
    at_edge = position == (0 if step > 0 else x - 1)
    return jnp.where(at_edge, jnp.concatenate([keys_part, values_part], axis=0), plain)


def swap_cores(block):
    devices = range(lax.axis_size("space"))
    return lax.ppermute(block, "space", [(i, i ^ 1) for i in devices])


def fetch_sources(stacked):
    frame_count = stacked.shape[1]
    earlier = tm_shift(stacked[:, frame_count - TR :], 1)
    following = tm_shift(stacked[:, :TR], -1)
    far_next = shifted(stacked, "space", -2)
    far_prev = shifted(stacked, "space", 2)
    core_zero = lax.axis_index("space") % 2 == 0
    near_next = swap_cores(jnp.where(core_zero, far_next, stacked))
    near_prev = swap_cores(jnp.where(core_zero, stacked, far_prev))
    early_band = earlier[:, TR - 1 :]
    late_band = following[:, :1]
    return (
        stacked, earlier, following, far_next, far_prev, near_next, near_prev,
        shifted(early_band, "space", -1), shifted(early_band, "space", 1),
        shifted(late_band, "space", -1), shifted(late_band, "space", 1),
    )


def locate(frame, d, e):
    offset = frame + d
    if e == 0:
        if offset < 0:
            return 1, offset + TR
        if offset < 2:
            return 0, offset
        return 2, offset - 2
    if abs(e) == 1:
        side = 0 if e > 0 else 1
        if offset < 0:
            return 7 + side, 0
        if offset < 2:
            return 5 + side, offset
        return 9 + side, 0
    return (3 if e > 0 else 4), frame


LOCAL = (0, 3, 4, 5, 6)
HEAD_GROUP = 4
REMOTE = (1, 2, 7, 8, 9, 10)


def scored_pairs(flags_ref, query, sources, frame, kept_sources, lanes):
    score_scale = 1.0 / math.sqrt(HD)
    score_list = []
    value_list = []
    for d, e in band_list():
        which, index = locate(frame, d, e)
        if which not in kept_sources:
            continue
        source = sources[kept_sources.index(which)]
        raw = (
            lax.dot_general(
                query, source[0, index, :, lanes], (((1,), (1,)), ((), ())),
                preferred_element_type=jnp.float32,
            )
            * score_scale
        )
        flag = flags_ref[frame * 25 + (TR + d) * 5 + (W + e)]
        score_list.append(jnp.where(flag > 0, raw, -jnp.inf))
        value_list.append(source[1, index, :, lanes])
    tile_max = score_list[0]
    for scores in score_list[1:]:
        tile_max = jnp.maximum(tile_max, scores)
    return score_list, value_list, jnp.max(tile_max, axis=1, keepdims=True)


def weighted_sums(score_list, value_list, row_max):
    tile_sum = jnp.zeros_like(score_list[0])
    summed = jnp.zeros((row_max.shape[0], HD), jnp.float32)
    for scores, value_tile in zip(score_list, value_list):
        weights = jnp.exp(scores - row_max)
        tile_sum = tile_sum + weights
        summed = summed + jnp.dot(
            weights.astype(jnp.bfloat16), value_tile, preferred_element_type=jnp.float32
        )
    return jnp.sum(tile_sum, axis=1, keepdims=True), summed


def local_kernel(flags_ref, q_ref, *refs):
    *sources, max_ref, sum_ref, acc_ref = refs
    for head in range(max_ref.shape[0]):
        lanes = slice(head * HD, (head + 1) * HD)
        for frame in range(q_ref.shape[0]):
            score_list, value_list, row_max = scored_pairs(
                flags_ref, q_ref[frame, :, lanes], sources, frame, LOCAL, lanes
            )
            denominator, summed = weighted_sums(score_list, value_list, row_max)
            max_ref[head, frame] = row_max
            sum_ref[head, frame] = denominator
            acc_ref[frame, :, lanes] = summed


def remote_kernel(flags_ref, q_ref, *refs):
    *sources, max_ref, sum_ref, acc_ref, o_ref = refs
    for head in range(max_ref.shape[0]):
        lanes = slice(head * HD, (head + 1) * HD)
        for frame in range(q_ref.shape[0]):
            score_list, value_list, remote_max = scored_pairs(
                flags_ref, q_ref[frame, :, lanes], sources, frame, REMOTE, lanes
            )
            local_max = max_ref[head, frame]
            row_max = jnp.maximum(local_max, remote_max)
            rescale = jnp.exp(local_max - row_max)
            denominator, summed = weighted_sums(score_list, value_list, row_max)
            denominator = denominator + rescale * sum_ref[head, frame]
            summed = summed + rescale * acc_ref[frame, :, lanes]
            o_ref[frame, :, lanes] = (summed / denominator).astype(o_ref.dtype)


def attend(queries, sources, tile_flags):
    frame_count, row_count, feature_width = queries.shape
    head_count = feature_width // HD
    group = HEAD_GROUP
    steps = head_count // group
    flags = tile_flags.reshape(-1).astype(jnp.int32)
    def source_spec(source):
        return pl.BlockSpec((2, source.shape[1], row_count, group * HD), lambda h, flags: (0, 0, 0, h))

    tile_spec = pl.BlockSpec((frame_count, row_count, group * HD), lambda h, flags: (0, 0, h))
    stat_spec = pl.BlockSpec((group, frame_count, row_count, 1), lambda h, flags: (h, 0, 0, 0))
    stat_shape = jax.ShapeDtypeStruct((head_count, frame_count, row_count, 1), jnp.float32)
    acc_shape = jax.ShapeDtypeStruct(queries.shape, jnp.float32)
    local_sources = [sources[i] for i in LOCAL]
    remote_sources = [sources[i] for i in REMOTE]

    def cost(count, extra):
        return pl.CostEstimate(
            flops=4 * frame_count * head_count * count * row_count * row_count * HD,
            transcendentals=frame_count * head_count * count * row_count * row_count,
            bytes_accessed=(2 + 4 * extra + 4) * frame_count * row_count * feature_width,
        )

    stats = pl.pallas_call(
        local_kernel,
        grid_spec=pltpu.PrefetchScalarGridSpec(
            num_scalar_prefetch=1,
            grid=(steps,),
            in_specs=[tile_spec] + [source_spec(s) for s in local_sources],
            out_specs=[stat_spec, stat_spec, tile_spec],
        ),
        out_shape=[stat_shape, stat_shape, acc_shape],
        cost_estimate=cost(16, len(local_sources)),
    )(flags, queries, *local_sources)
    return pl.pallas_call(
        remote_kernel,
        grid_spec=pltpu.PrefetchScalarGridSpec(
            num_scalar_prefetch=1,
            grid=(steps,),
            in_specs=[tile_spec] + [source_spec(s) for s in remote_sources]
            + [stat_spec, stat_spec, tile_spec],
            out_specs=tile_spec,
        ),
        out_shape=jax.ShapeDtypeStruct(queries.shape, queries.dtype),
        cost_estimate=cost(10, len(remote_sources)),
    )(flags, queries, *remote_sources, *stats)


def on_device(queries, keys, values, tile_mask):
    stacked = jnp.stack([keys, values], 0)
    sources = fetch_sources(stacked)
    tile_flags = tile_mask[:, 0]
    return attend(queries, sources, tile_flags)


def solution(mesh):
    in_specs = (
        P("tm", "space", None),
        P("tm", "space", None),
        P("tm", "space", None),
        P("tm", "space", None, None),
    )
    out_specs = P("tm", "space", None)
    return jax.shard_map(
        on_device, mesh=mesh, in_specs=in_specs, out_specs=out_specs, check_vma=False
    )
```

```python
import math

import jax
import jax.numpy as jnp
from jax import lax
from jax.experimental import pallas as pl
from jax.experimental.pallas import tpu as pltpu
from jax.sharding import PartitionSpec as P

HD = 128
TR = 2
W = 2


def shifted(block, axis, distance):
    devices = range(lax.axis_size(axis))
    route = [(i - distance, i) for i in devices if i - distance in devices]
    return lax.ppermute(block, axis, route)


def band_list():
    pairs = []
    for d in range(-TR, TR + 1):
        spread = W >> abs(d)
        for e in range(-spread, spread + 1):
            pairs.append((d, e))
    return pairs


def frame_reach(e):
    best = 0
    for d in range(TR + 1):
        if W >> d >= abs(e):
            best = d
    return best


X_CHIPS = 4


def routed(pairs, block):
    return lax.ppermute(block, "tm", pairs) if pairs else jnp.zeros_like(block)


def relayed(block, hops):
    for pairs in hops:
        block = routed(pairs, block)
    return block


def tm_shift(block, step):
    count = lax.axis_size("tm")
    x = X_CHIPS
    if step > 0:
        edge = [t for t in range(count - 1) if t % x == x - 1]
        direct = [(t, t + 1) for t in range(count - 1) if t not in edge]
        via_two = [[(t, t - 1) for t in edge], [(t - 1, t + 3) for t in edge], [(t + 3, t + 1) for t in edge]]
        via_one = [[(t, t - 2) for t in edge], [(t - 2, t + 2) for t in edge], [(t + 2, t + 1) for t in edge]]
    else:
        edge = [t for t in range(1, count) if t % x == 0]
        direct = [(t, t - 1) for t in range(1, count) if t not in edge]
        via_one = [[(t, t + 1) for t in edge], [(t + 1, t - 3) for t in edge], [(t - 3, t - 1) for t in edge]]
        via_two = [[(t, t + 2) for t in edge], [(t + 2, t - 2) for t in edge], [(t - 2, t - 1) for t in edge]]
    plain = routed(direct, block)
    keys_part = relayed(block[:1], via_one)
    values_part = relayed(block[1:], via_two)
    position = lax.axis_index("tm") % x
    at_edge = position == (0 if step > 0 else x - 1)
    return jnp.where(at_edge, jnp.concatenate([keys_part, values_part], axis=0), plain)


def swap_cores(block):
    devices = range(lax.axis_size("space"))
    return lax.ppermute(block, "space", [(i, i ^ 1) for i in devices])


def fetch_sources(stacked):
    frame_count = stacked.shape[1]
    earlier = tm_shift(stacked[:, frame_count - TR :], 1)
    following = tm_shift(stacked[:, :TR], -1)
    far_next = shifted(stacked, "space", -2)
    far_prev = shifted(stacked, "space", 2)
    core_zero = lax.axis_index("space") % 2 == 0
    partner_own = swap_cores(stacked)
    partner_far = swap_cores(jnp.where(core_zero, far_next, far_prev))
    near_next = jnp.where(core_zero, partner_own, partner_far)
    near_prev = jnp.where(core_zero, partner_far, partner_own)
    early_band = earlier[:, TR - 1 :]
    late_band = following[:, :1]
    return (
        stacked, earlier, following, far_next, far_prev, near_next, near_prev,
        shifted(early_band, "space", -1), shifted(early_band, "space", 1),
        shifted(late_band, "space", -1), shifted(late_band, "space", 1),
    )


def locate(frame, d, e):
    offset = frame + d
    if e == 0:
        if offset < 0:
            return 1, offset + TR
        if offset < 2:
            return 0, offset
        return 2, offset - 2
    if abs(e) == 1:
        side = 0 if e > 0 else 1
        if offset < 0:
            return 7 + side, 0
        if offset < 2:
            return 5 + side, offset
        return 9 + side, 0
    return (3 if e > 0 else 4), frame


LOCAL = (0, 3, 4, 5, 6)
HEAD_GROUP = 6
REMOTE = (1, 2, 7, 8, 9, 10)


def scored_pairs(flags_ref, query, sources, frame, kept_sources, lanes):
    score_scale = 1.0 / math.sqrt(HD)
    score_list = []
    value_list = []
    for d, e in band_list():
        which, index = locate(frame, d, e)
        if which not in kept_sources:
            continue
        source = sources[kept_sources.index(which)]
        raw = (
            lax.dot_general(
                query, source[0, index, :, lanes], (((1,), (1,)), ((), ())),
                preferred_element_type=jnp.float32,
            )
            * score_scale
        )
        flag = flags_ref[frame * 25 + (TR + d) * 5 + (W + e)]
        score_list.append(jnp.where(flag > 0, raw, -jnp.inf))
        value_list.append(source[1, index, :, lanes])
    tile_max = score_list[0]
    for scores in score_list[1:]:
        tile_max = jnp.maximum(tile_max, scores)
    return score_list, value_list, jnp.max(tile_max, axis=1, keepdims=True)


def weighted_sums(score_list, value_list, row_max):
    tile_sum = jnp.zeros_like(score_list[0])
    summed = jnp.zeros((row_max.shape[0], HD), jnp.float32)
    for scores, value_tile in zip(score_list, value_list):
        weights = jnp.exp(scores - row_max)
        tile_sum = tile_sum + weights
        summed = summed + jnp.dot(
            weights.astype(jnp.bfloat16), value_tile, preferred_element_type=jnp.float32
        )
    return jnp.sum(tile_sum, axis=1, keepdims=True), summed


def local_kernel(flags_ref, q_ref, *refs):
    *sources, max_ref, sum_ref, acc_ref = refs
    for head in range(max_ref.shape[0]):
        lanes = slice(head * HD, (head + 1) * HD)
        for frame in range(q_ref.shape[0]):
            score_list, value_list, row_max = scored_pairs(
                flags_ref, q_ref[frame, :, lanes], sources, frame, LOCAL, lanes
            )
            denominator, summed = weighted_sums(score_list, value_list, row_max)
            max_ref[head, frame] = row_max
            sum_ref[head, frame] = denominator
            acc_ref[frame, :, lanes] = summed


def remote_kernel(flags_ref, q_ref, *refs):
    *sources, max_ref, sum_ref, acc_ref, o_ref = refs
    for head in range(max_ref.shape[0]):
        lanes = slice(head * HD, (head + 1) * HD)
        for frame in range(q_ref.shape[0]):
            score_list, value_list, remote_max = scored_pairs(
                flags_ref, q_ref[frame, :, lanes], sources, frame, REMOTE, lanes
            )
            local_max = max_ref[head, frame]
            row_max = jnp.maximum(local_max, remote_max)
            rescale = jnp.exp(local_max - row_max)
            denominator, summed = weighted_sums(score_list, value_list, row_max)
            denominator = denominator + rescale * sum_ref[head, frame]
            summed = summed + rescale * acc_ref[frame, :, lanes]
            o_ref[frame, :, lanes] = (summed / denominator).astype(o_ref.dtype)


def attend(queries, sources, tile_flags):
    frame_count, row_count, feature_width = queries.shape
    head_count = feature_width // HD
    group = HEAD_GROUP
    steps = head_count // group
    flags = tile_flags.reshape(-1).astype(jnp.int32)
    def source_spec(source):
        return pl.BlockSpec((2, source.shape[1], row_count, group * HD), lambda h, flags: (0, 0, 0, h))

    tile_spec = pl.BlockSpec((frame_count, row_count, group * HD), lambda h, flags: (0, 0, h))
    stat_spec = pl.BlockSpec((group, frame_count, row_count, 1), lambda h, flags: (h, 0, 0, 0))
    stat_shape = jax.ShapeDtypeStruct((head_count, frame_count, row_count, 1), jnp.float32)
    acc_shape = jax.ShapeDtypeStruct(queries.shape, jnp.float32)
    local_sources = [sources[i] for i in LOCAL]
    remote_sources = [sources[i] for i in REMOTE]

    def cost(count, extra):
        return pl.CostEstimate(
            flops=4 * frame_count * head_count * count * row_count * row_count * HD,
            transcendentals=frame_count * head_count * count * row_count * row_count,
            bytes_accessed=(2 + 4 * extra + 4) * frame_count * row_count * feature_width,
        )

    stats = pl.pallas_call(
        local_kernel,
        grid_spec=pltpu.PrefetchScalarGridSpec(
            num_scalar_prefetch=1,
            grid=(steps,),
            in_specs=[tile_spec] + [source_spec(s) for s in local_sources],
            out_specs=[stat_spec, stat_spec, tile_spec],
        ),
        out_shape=[stat_shape, stat_shape, acc_shape],
        cost_estimate=cost(16, len(local_sources)),
    )(flags, queries, *local_sources)
    return pl.pallas_call(
        remote_kernel,
        grid_spec=pltpu.PrefetchScalarGridSpec(
            num_scalar_prefetch=1,
            grid=(steps,),
            in_specs=[tile_spec] + [source_spec(s) for s in remote_sources]
            + [stat_spec, stat_spec, tile_spec],
            out_specs=tile_spec,
        ),
        out_shape=jax.ShapeDtypeStruct(queries.shape, queries.dtype),
        cost_estimate=cost(10, len(remote_sources)),
    )(flags, queries, *remote_sources, *stats)


def on_device(queries, keys, values, tile_mask):
    stacked = jnp.stack([keys, values], 0)
    sources = fetch_sources(stacked)
    tile_flags = tile_mask[:, 0]
    return attend(queries, sources, tile_flags)


def solution(mesh):
    in_specs = (
        P("tm", "space", None),
        P("tm", "space", None),
        P("tm", "space", None),
        P("tm", "space", None, None),
    )
    out_specs = P("tm", "space", None)
    return jax.shard_map(
        on_device, mesh=mesh, in_specs=in_specs, out_specs=out_specs, check_vma=False
    )
```
